512 devices in a mesh: chan: 32 (over y, z_lo), inp: 16 (over z_hi, x, core).
Axes of the slice: x: 4, y: 4, z: 16 (z_hi: 2, z_lo: 8; z = z_hi * 8 + z_lo), core: 2. Of those that a mesh axis runs over, the one named last changes fastest.
Arguments:
- voltages: int32 [512, 524288], P('inp', 'chan'), may hold values from -128 to 127
- scales: int32 [512], P('inp'), may hold values from 1 to 5
Outputs:
- visibilities: bfloat16 [2, 1024, 512, 512], P(None, 'chan', 'inp')
The draws below stay inside these ranges and needn't reach their ends.
All inputs are finite; a program needn't handle non-finite values.
Results may differ from the reference program's by a relative error of at most 0.0069.
Values may be sent and summed in bfloat16 or wider, within the bound.
No kernel may reach another device: no remote copies, remote signals or barrier semaphores. Data moves between devices by JAX's collectives and lax.ppermute only.
A program may use at most 128 MiB of HBM per device.

```python
import math
import jax
import jax.numpy as jnp
from jax import lax

INPUTS = 512
NFFT = 4096
CHANS = 1024
TAPS = 8
SPECTRA = 128


def touch_ends(values, stream_key, low, largest):
    shape = values.shape
    place = [jax.random.randint(jax.random.fold_in(stream_key, axis), (), 0, shape[axis]) for axis in range(len(shape))]
    values = values.at[tuple(place)].set(low)
    longest = shape.index(max(shape))
    place[longest] = (place[longest] + 1) % shape[longest]
    return values.at[tuple(place)].set(largest)


def setup_inputs(seed: int = 0) -> dict:
    key_of = jax.random.split(jax.random.key(seed), 3)
    return {
        "voltages": touch_ends(jax.random.randint(key_of[0], (INPUTS, SPECTRA * NFFT), -128, 128), jax.random.fold_in(key_of[0], 1), -128, 127).astype(jnp.int32),
        "scales": touch_ends(jax.random.randint(key_of[1], (INPUTS,), 1, 6), jax.random.fold_in(key_of[1], 1), 1, 5).astype(jnp.int32),
    }


def window_table():
    count = TAPS * NFFT
    places = jnp.arange(count).astype(jnp.float32)
    shaping = jnp.sinc((places - count / 2.0) / NFFT)
    taper = 0.5 - 0.5 * jnp.cos(2.0 * math.pi * places / count)
    return (shaping * taper).reshape(TAPS, NFFT)

def dft_table():
    columns = jnp.arange(CHANS, dtype=jnp.int32)
    norm_factor = 1.0 / math.sqrt(NFFT)

    def one_block(start):
        rows_idx = start + jnp.arange(512, dtype=jnp.int32)
        phase = rows_idx[:, None] * columns[None, :] % NFFT
        angle = phase.astype(jnp.float32) * (2.0 * math.pi / NFFT)
        return jnp.stack([jnp.cos(angle) * norm_factor, -jnp.sin(angle) * norm_factor], axis=1).astype(jnp.bfloat16)
    starts = jnp.arange(NFFT // 512, dtype=jnp.int32) * 512
    return lax.map(one_block, starts).reshape(NFFT, 2, CHANS)

def filter_taps(padded, window, spec_count):
    total = jnp.zeros((padded.shape[0], spec_count, NFFT), jnp.float32)
    for tap_index in range(TAPS):
        total = total + window[tap_index] * padded[:, tap_index:tap_index + spec_count]
    return total.astype(jnp.bfloat16)

def reference(voltages, scales):
    window = window_table()
    table = dft_table()
    group = 32
    volt_groups = voltages.reshape(INPUTS // group, group, SPECTRA, NFFT)
    scale_groups = scales.reshape(INPUTS // group, group)

    def one_group(operands):
        volt_block, scale_block = operands
        signal = volt_block.astype(jnp.float32) * scale_block.astype(jnp.float32)[:, None, None] * (1.0 / 256.0)
        padded = jnp.concatenate([jnp.zeros((group, TAPS - 1, NFFT), jnp.float32), signal], axis=1)
        filtered = filter_taps(padded, window, SPECTRA)
        return jnp.einsum('isn,nrc->cirs', filtered.astype(jnp.float32), table.astype(jnp.float32)).astype(jnp.bfloat16)
    parts = lax.map(one_group, (volt_groups, scale_groups))
    spectra = jnp.moveaxis(parts, 0, 1).reshape(CHANS, INPUTS, 2 * SPECTRA)
    blocks = spectra.reshape(CHANS // 8, 8, INPUTS, 2 * SPECTRA)

    def correlate(block):
        values = block.astype(jnp.float32)
        swapped = jnp.concatenate([values[..., SPECTRA:], -values[..., :SPECTRA]], axis=-1)
        real_part = jnp.einsum('cik,cjk->cij', values, values) * (1.0 / SPECTRA)
        imag_part = jnp.einsum('cik,cjk->cij', swapped, values) * (1.0 / SPECTRA)
        return (real_part.astype(jnp.bfloat16), imag_part.astype(jnp.bfloat16))
    real_all, imag_all = lax.map(correlate, blocks)
    return jnp.stack([real_all.reshape(CHANS, INPUTS, INPUTS), imag_all.reshape(CHANS, INPUTS, INPUTS)])
```

```python
import math

import jax
import jax.numpy as jnp
from jax import lax
from jax.sharding import PartitionSpec as P

NFFT = 4096
CHANS = 1024
TAPS = 8
ROOT = 64


def shifted(block, axis, distance):
    devices = range(lax.axis_size(axis))
    route = [(i - distance, i) for i in devices if i - distance in devices]
    return lax.ppermute(block, axis, route)


def moved(block, mapping):
    return lax.ppermute(block, "inp", [(p, mapping(p)) for p in range(lax.axis_size("inp"))])


def window_table():
    count = TAPS * NFFT
    places = jnp.arange(count).astype(jnp.float32)
    shaping = jnp.sinc((places - count / 2.0) / NFFT)
    taper = 0.5 - 0.5 * jnp.cos(2.0 * math.pi * places / count)
    return (shaping * taper).reshape(TAPS, NFFT)


def dft_table():
    columns = jnp.arange(CHANS, dtype=jnp.int32)
    rows = jnp.arange(ROOT, dtype=jnp.int32)
    step = 2.0 * math.pi / NFFT

    def factor(scale):
        angle = ((scale * rows[:, None] * columns[None, :]) % NFFT).astype(jnp.float32) * step
        return jnp.cos(angle), -jnp.sin(angle)

    hr, hi = factor(ROOT)
    lr, li = factor(1)
    real = hr[:, None, :] * lr[None, :, :] - hi[:, None, :] * li[None, :, :]
    imag = hr[:, None, :] * li[None, :, :] + hi[:, None, :] * lr[None, :, :]
    both = jnp.stack([real, imag], axis=2) * (1.0 / math.sqrt(NFFT))
    return both.astype(jnp.bfloat16).reshape(NFFT, 2 * CHANS)


def gather_inputs(own):
    assert lax.axis_size("inp") == 16
    me = lax.axis_index("inp")
    zh, xx, core = me // 8, (me // 2) % 4, me % 2

    def at(z, x, c):
        return z * 8 + (x % 4) * 2 + c

    def unpack(p):
        return p // 8, (p // 2) % 4, p % 2

    def x_step(d):
        def f(p):
            z, x, c = unpack(p)
            return at(z, x + d, c)
        return f

    cross = moved(own, lambda p: p ^ 8)
    from_left = moved((own, cross), x_step(1))
    from_right = moved((own, cross), x_step(-1))
    far_own = moved(from_left[0], x_step(1))
    far_cross = moved(from_right[1], x_step(-1))
    mine = [
        (0, 0, own), (1, 0, cross),
        (0, -1, from_left[0]), (1, -1, from_left[1]),
        (0, 1, from_right[0]), (1, 1, from_right[1]),
        (0, 2, far_own), (1, 2, far_cross),
    ]
    other = moved(tuple(b for _, _, b in mine), lambda p: p ^ 1)
    width = own.shape[1]
    gathered = jnp.zeros((own.shape[0], 16 * width, own.shape[2]), own.dtype)
    for (dz, dx, block), far in zip(mine, other):
        for dc, piece in ((0, block), (1, far)):
            place = at((zh + dz) % 2, xx + dx + 4, (core + dc) % 2)
            gathered = lax.dynamic_update_slice(gathered, piece, (0, place * width, 0))
    return gathered


def shards(voltages, scales):
    inp_count = voltages.shape[0]
    shard_len = voltages.shape[1]
    spec_count = shard_len // NFFT
    history = TAPS - 1
    samples = voltages.reshape(inp_count, spec_count, NFFT).transpose(1, 0, 2).astype(jnp.bfloat16)
    earlier = []
    need = history
    distance = 1
    while need > 0:
        take = min(spec_count, need)
        earlier = [shifted(samples[spec_count - take :], "chan", distance)] + earlier
        need -= take
        distance += 1
    joined = jnp.concatenate(earlier + [samples], axis=0).astype(jnp.float32)
    signal = joined * (scales.astype(jnp.float32) * (1.0 / 256.0))[None, :, None]
    window = window_table()
    total = jnp.zeros((spec_count, inp_count, NFFT), jnp.float32)
    for tap in range(TAPS):
        total = total + window[tap] * signal[tap : tap + spec_count]
    filtered = total.astype(jnp.bfloat16).reshape(spec_count * inp_count, NFFT)
    spectra = jnp.dot(filtered, dft_table(), preferred_element_type=jnp.float32).astype(jnp.bfloat16)
    spectra = spectra.reshape(spec_count, inp_count, 2, CHANS)
    local_block = lax.all_to_all(spectra, "chan", split_axis=3, concat_axis=0, tiled=True)
    spec_total = local_block.shape[0]
    chan_count = local_block.shape[3]
    own_rows = local_block.transpose(3, 1, 2, 0).reshape(chan_count, inp_count, 2 * spec_total)
    swapped = jnp.concatenate([own_rows[..., spec_total:], -own_rows[..., :spec_total]], axis=-1)
    piece = gather_inputs(own_rows)
    real_part = jnp.einsum("cik,cjk->cij", own_rows, piece, preferred_element_type=jnp.float32)
    imag_part = jnp.einsum("cik,cjk->cij", swapped, piece, preferred_element_type=jnp.float32)
    result = jnp.stack([real_part, imag_part]) * (1.0 / spec_total)
    return result.astype(jnp.bfloat16)


def solution(mesh):
    placed = (P("inp", "chan"), P("inp"))
    return jax.shard_map(
        shards, mesh=mesh, in_specs=placed, out_specs=P(None, "chan", "inp", None), check_vma=False
    )
```

```python
import functools
import math

import jax
import jax.numpy as jnp
from jax import lax
from jax.experimental import pallas as pl
from jax.sharding import PartitionSpec as P

NFFT = 4096
CHANS = 1024
TAPS = 8
ROOT = 64


def shifted(block, axis, distance):
    devices = range(lax.axis_size(axis))
    route = [(i - distance, i) for i in devices if i - distance in devices]
    return lax.ppermute(block, axis, route)


def moved(block, mapping):
    return lax.ppermute(block, "inp", [(p, mapping(p)) for p in range(lax.axis_size("inp"))])


def window_table():
    count = TAPS * NFFT
    places = jnp.arange(count).astype(jnp.float32)
    shaping = jnp.sinc((places - count / 2.0) / NFFT)
    taper = 0.5 - 0.5 * jnp.cos(2.0 * math.pi * places / count)
    return (shaping * taper).reshape(TAPS, NFFT)


def dft_table():
    columns = jnp.arange(CHANS, dtype=jnp.int32)
    rows = jnp.arange(ROOT, dtype=jnp.int32)
    step = 2.0 * math.pi / NFFT

    def factor(scale):
        angle = ((scale * rows[:, None] * columns[None, :]) % NFFT).astype(jnp.float32) * step
        return jnp.cos(angle), -jnp.sin(angle)

    def spread(part, axis):
        grown = jnp.broadcast_to(jnp.expand_dims(part, axis), (ROOT, ROOT, CHANS))
        return grown.reshape(NFFT, CHANS)

    hr, hi = (spread(t, 1) for t in factor(ROOT))
    lr, li = (spread(t, 0) for t in factor(1))
    real = hr * lr - hi * li
    imag = hr * li + hi * lr
    both = jnp.concatenate([real, imag], axis=1) * (1.0 / math.sqrt(NFFT))
    return lax.optimization_barrier(both.astype(jnp.bfloat16))


def polyphase_kernel(spec_count, x_ref, w_ref, g_ref, o_ref):
    gain = g_ref[...]
    for s in range(spec_count):
        total = jnp.zeros(o_ref.shape[1:], jnp.float32)
        for tap in range(TAPS):
            total = total + w_ref[tap : tap + 1, :] * (x_ref[s + tap].astype(jnp.float32) * gain)
        o_ref[s] = total.astype(o_ref.dtype)


def polyphase(joined, window, gain, spec_count):
    rows, inputs, length = joined.shape
    lanes = 512
    return pl.pallas_call(
        functools.partial(polyphase_kernel, spec_count),
        out_shape=jax.ShapeDtypeStruct((spec_count, inputs, length), jnp.bfloat16),
        grid=(length // lanes,),
        in_specs=[
            pl.BlockSpec((rows, inputs, lanes), lambda k: (0, 0, k)),
            pl.BlockSpec((TAPS, lanes), lambda k: (0, k)),
            pl.BlockSpec((inputs, 1), lambda k: (0, 0)),
        ],
        out_specs=pl.BlockSpec((spec_count, inputs, lanes), lambda k: (0, 0, k)),
    )(joined, window, gain)


def gather_inputs(own):
    assert lax.axis_size("inp") == 16
    me = lax.axis_index("inp")
    zh, xx, core = me // 8, (me // 2) % 4, me % 2

    def at(z, x, c):
        return z * 8 + (x % 4) * 2 + c

    def unpack(p):
        return p // 8, (p // 2) % 4, p % 2

    def x_step(d):
        def f(p):
            z, x, c = unpack(p)
            return at(z, x + d, c)
        return f

    cross = moved(own, lambda p: p ^ 8)
    from_left = moved((own, cross), x_step(1))
    from_right = moved((own, cross), x_step(-1))
    far_own = moved(from_left[0], x_step(1))
    far_cross = moved(from_right[1], x_step(-1))
    mine = [
        (0, 0, own), (1, 0, cross),
        (0, -1, from_left[0]), (1, -1, from_left[1]),
        (0, 1, from_right[0]), (1, 1, from_right[1]),
        (0, 2, far_own), (1, 2, far_cross),
    ]
    other = moved(tuple(b for _, _, b in mine), lambda p: p ^ 1)
    width = own.shape[1]
    gathered = jnp.zeros((own.shape[0], 16 * width, own.shape[2]), own.dtype)
    for (dz, dx, block), far in zip(mine, other):
        for dc, piece in ((0, block), (1, far)):
            place = at((zh + dz) % 2, xx + dx + 4, (core + dc) % 2)
            gathered = lax.dynamic_update_slice(gathered, piece, (0, place * width, 0))
    return gathered


def shards(voltages, scales):
    inp_count = voltages.shape[0]
    shard_len = voltages.shape[1]
    spec_count = shard_len // NFFT
    history = TAPS - 1
    samples = voltages.reshape(inp_count, spec_count, NFFT).transpose(1, 0, 2).astype(jnp.bfloat16)
    earlier = []
    need = history
    distance = 1
    while need > 0:
        take = min(spec_count, need)
        earlier = [shifted(samples[spec_count - take :], "chan", distance)] + earlier
        need -= take
        distance += 1
    joined = jnp.concatenate(earlier + [samples], axis=0)
    gain = (scales.astype(jnp.float32) * (1.0 / 256.0)).reshape(inp_count, 1)
    filtered = polyphase(joined, window_table(), gain, spec_count).reshape(spec_count * inp_count, NFFT)
    spectra = jnp.dot(filtered, dft_table(), preferred_element_type=jnp.float32).astype(jnp.bfloat16)
    spectra = spectra.reshape(spec_count, inp_count, 2, CHANS)
    local_block = lax.all_to_all(spectra, "chan", split_axis=3, concat_axis=0, tiled=True)
    spec_total = local_block.shape[0]
    chan_count = local_block.shape[3]
    own_rows = local_block.transpose(3, 1, 2, 0).reshape(chan_count, inp_count, 2 * spec_total)
    swapped = jnp.concatenate([own_rows[..., spec_total:], -own_rows[..., :spec_total]], axis=-1)
    piece = gather_inputs(own_rows)
    real_part = jnp.einsum("cik,cjk->cij", own_rows, piece, preferred_element_type=jnp.float32)
    imag_part = jnp.einsum("cik,cjk->cij", swapped, piece, preferred_element_type=jnp.float32)
    result = jnp.stack([real_part, imag_part]) * (1.0 / spec_total)
    return result.astype(jnp.bfloat16)


def solution(mesh):
    placed = (P("inp", "chan"), P("inp"))
    return jax.shard_map(
        shards, mesh=mesh, in_specs=placed, out_specs=P(None, "chan", "inp", None), check_vma=False
    )
```

```python
import functools
import math

import jax
import jax.numpy as jnp
from jax import lax
from jax.experimental import pallas as pl
from jax.sharding import PartitionSpec as P

NFFT = 4096
CHANS = 1024
TAPS = 8
ROOT = 64


def shifted(block, axis, distance):
    devices = range(lax.axis_size(axis))
    route = [(i - distance, i) for i in devices if i - distance in devices]
    return lax.ppermute(block, axis, route)


def moved(block, mapping):
    return lax.ppermute(block, "inp", [(p, mapping(p)) for p in range(lax.axis_size("inp"))])


def window_table():
    count = TAPS * NFFT
    places = jnp.arange(count).astype(jnp.float32)
    shaping = jnp.sinc((places - count / 2.0) / NFFT)
    taper = 0.5 - 0.5 * jnp.cos(2.0 * math.pi * places / count)
    return (shaping * taper).reshape(TAPS, NFFT)


def dft_table():
    columns = jnp.arange(CHANS, dtype=jnp.int32)
    rows = jnp.arange(ROOT, dtype=jnp.int32)
    step = 2.0 * math.pi / NFFT

    def factor(scale):
        angle = ((scale * rows[:, None] * columns[None, :]) % NFFT).astype(jnp.float32) * step
        return jnp.cos(angle), -jnp.sin(angle)

    def spread(part, axis):
        grown = jnp.broadcast_to(jnp.expand_dims(part, axis), (ROOT, ROOT, CHANS))
        return grown.reshape(NFFT, CHANS)

    hr, hi = (spread(t, 1) for t in factor(ROOT))
    lr, li = (spread(t, 0) for t in factor(1))
    real = hr * lr - hi * li
    imag = hr * li + hi * lr
    both = jnp.concatenate([real, imag], axis=1) * (1.0 / math.sqrt(NFFT))
    return lax.optimization_barrier(both.astype(jnp.bfloat16))


def polyphase_kernel(spec_count, x_ref, w_ref, g_ref, o_ref):
    gain = g_ref[...]
    for s in range(spec_count):
        total = jnp.zeros(o_ref.shape[1:], jnp.float32)
        for tap in range(TAPS):
            total = total + w_ref[tap : tap + 1, :] * (x_ref[s + tap].astype(jnp.float32) * gain)
        o_ref[s] = total.astype(o_ref.dtype)


def polyphase(joined, window, gain, spec_count):
    rows, inputs, length = joined.shape
    lanes = 512
    return pl.pallas_call(
        functools.partial(polyphase_kernel, spec_count),
        out_shape=jax.ShapeDtypeStruct((spec_count, inputs, length), jnp.bfloat16),
        grid=(length // lanes,),
        in_specs=[
            pl.BlockSpec((rows, inputs, lanes), lambda k: (0, 0, k)),
            pl.BlockSpec((TAPS, lanes), lambda k: (0, k)),
            pl.BlockSpec((inputs, 1), lambda k: (0, 0)),
        ],
        out_specs=pl.BlockSpec((spec_count, inputs, lanes), lambda k: (0, 0, k)),
    )(joined, window, gain)


def place_of():
    assert lax.axis_size("inp") == 16
    me = lax.axis_index("inp")
    return me // 8, (me // 2) % 4, me % 2


def x_step(d):
    return lambda p: (p // 8) * 8 + ((p // 2 + d) % 4) * 2 + p % 2


def column_blocks(pair, zh, xx):
    chans, width, depth = pair.shape[0], pair.shape[1] // 2, pair.shape[2]
    from_left = moved(pair, x_step(1))
    from_right = moved(pair, x_step(-1))
    far_low = moved(from_left[:, :width], x_step(1))
    far_high = moved(from_right[:, width:], x_step(-1))
    pieces = [
        (0, 0, pair[:, :width]), (1, 0, pair[:, width:]),
        (0, -1, from_left[:, :width]), (1, -1, from_left[:, width:]),
        (0, 1, from_right[:, :width]), (1, 1, from_right[:, width:]),
        (0, 2, far_low), (1, 2, far_high),
    ]
    column = jnp.zeros((chans, 8 * width, depth), pair.dtype)
    for z, dx, piece in pieces:
        slot = z * 4 + (xx + dx + 4) % 4
        column = lax.dynamic_update_slice(column, piece, (0, slot * width, 0))
    return column


def shards(voltages, scales):
    inp_count = voltages.shape[0]
    shard_len = voltages.shape[1]
    spec_count = shard_len // NFFT
    history = TAPS - 1
    zh, xx, core = place_of()
    samples = voltages.reshape(inp_count, spec_count, NFFT).transpose(1, 0, 2).astype(jnp.bfloat16)
    earlier = []
    need = history
    distance = 1
    while need > 0:
        take = min(spec_count, need)
        earlier = [shifted(samples[spec_count - take :], "chan", distance)] + earlier
        need -= take
        distance += 1
    joined = jnp.concatenate(earlier + [samples], axis=0)
    gain = (scales.astype(jnp.float32) * (1.0 / 256.0)).reshape(inp_count, 1)
    filtered = polyphase(joined, window_table(), gain, spec_count).reshape(spec_count * inp_count, NFFT)
    spectra = jnp.dot(filtered, dft_table(), preferred_element_type=jnp.float32).astype(jnp.bfloat16)
    spectra = spectra.reshape(spec_count, inp_count, 2, CHANS)
    crossed = moved(spectra, lambda p: p ^ 8)
    low_first = zh == 0
    both = jnp.concatenate(
        [jnp.where(low_first, spectra, crossed), jnp.where(low_first, crossed, spectra)], axis=1
    )
    local_block = lax.all_to_all(both, "chan", split_axis=3, concat_axis=0, tiled=True)
    spec_total = local_block.shape[0]
    chan_count = local_block.shape[3]
    pair = local_block.transpose(3, 1, 2, 0).reshape(chan_count, 2 * inp_count, 2 * spec_total)
    own_rows = lax.dynamic_slice_in_dim(pair, zh * inp_count, inp_count, axis=1)
    swapped = jnp.concatenate([own_rows[..., spec_total:], -own_rows[..., :spec_total]], axis=-1)
    lhs = jnp.stack([own_rows, swapped])
    mine = column_blocks(pair, zh, xx)
    theirs = moved(mine, lambda p: p ^ 1)

    def correlate(column):
        return jnp.einsum("rcik,cjk->rcij", lhs, column, preferred_element_type=jnp.float32)

    part_mine = correlate(mine)
    part_theirs = correlate(theirs)
    first = jnp.where(core == 0, part_mine, part_theirs)
    second = jnp.where(core == 0, part_theirs, part_mine)
    shape = first.shape[:3] + (8, inp_count)
    result = jnp.stack([first.reshape(shape), second.reshape(shape)], axis=4)
    result = result.reshape(first.shape[:3] + (16 * inp_count,)) * (1.0 / spec_total)
    return result.astype(jnp.bfloat16)


def solution(mesh):
    placed = (P("inp", "chan"), P("inp"))
    return jax.shard_map(
        shards, mesh=mesh, in_specs=placed, out_specs=P(None, "chan", "inp", None), check_vma=False
    )
```

```python
import functools
import math

import jax
import jax.numpy as jnp
from jax import lax
from jax.experimental import pallas as pl
from jax.sharding import Mesh, NamedSharding, PartitionSpec as P

NFFT = 4096
CHANS = 1024
TAPS = 8
ROOT = 64


TIME = ("y", "zl")
INPUT = ("zh", "x", "core")


def shifted(block, axis, distance):
    devices = range(lax.axis_size(axis))
    route = [(i - distance, i) for i in devices if i - distance in devices]
    return lax.ppermute(block, axis, route)


def moved(block, mapping):
    return lax.ppermute(block, INPUT, [(p, mapping(p)) for p in range(lax.axis_size(INPUT))])


def window_table():
    count = TAPS * NFFT
    places = jnp.arange(count).astype(jnp.float32)
    shaping = jnp.sinc((places - count / 2.0) / NFFT)
    taper = 0.5 - 0.5 * jnp.cos(2.0 * math.pi * places / count)
    return (shaping * taper).reshape(TAPS, NFFT)


def dft_table():
    columns = jnp.arange(CHANS, dtype=jnp.int32)
    rows = jnp.arange(ROOT, dtype=jnp.int32)
    step = 2.0 * math.pi / NFFT

    def factor(scale):
        angle = ((scale * rows[:, None] * columns[None, :]) % NFFT).astype(jnp.float32) * step
        return jnp.cos(angle), -jnp.sin(angle)

    def spread(part, axis):
        grown = jnp.broadcast_to(jnp.expand_dims(part, axis), (ROOT, ROOT, CHANS))
        return grown.reshape(NFFT, CHANS)

    hr, hi = (spread(t, 1) for t in factor(ROOT))
    lr, li = (spread(t, 0) for t in factor(1))
    real = hr * lr - hi * li
    imag = hr * li + hi * lr
    both = jnp.concatenate([real, imag], axis=1) * (1.0 / math.sqrt(NFFT))
    return lax.optimization_barrier(both.astype(jnp.bfloat16))


def polyphase_kernel(spec_count, x_ref, w_ref, g_ref, o_ref):
    gain = g_ref[...]
    for s in range(spec_count):
        total = jnp.zeros(o_ref.shape[1:], jnp.float32)
        for tap in range(TAPS):
            total = total + w_ref[tap : tap + 1, :] * (x_ref[s + tap].astype(jnp.float32) * gain)
        o_ref[s] = total.astype(o_ref.dtype)


def polyphase(joined, window, gain, spec_count):
    rows, inputs, length = joined.shape
    lanes = 512
    return pl.pallas_call(
        functools.partial(polyphase_kernel, spec_count),
        out_shape=jax.ShapeDtypeStruct((spec_count, inputs, length), jnp.bfloat16),
        grid=(length // lanes,),
        in_specs=[
            pl.BlockSpec((rows, inputs, lanes), lambda k: (0, 0, k)),
            pl.BlockSpec((TAPS, lanes), lambda k: (0, k)),
            pl.BlockSpec((inputs, 1), lambda k: (0, 0)),
        ],
        out_specs=pl.BlockSpec((spec_count, inputs, lanes), lambda k: (0, 0, k)),
    )(joined, window, gain)


def gather_inputs(own):
    assert lax.axis_size(INPUT) == 16
    me = lax.axis_index(INPUT)
    zh, xx, core = me // 8, (me // 2) % 4, me % 2

    def at(z, x, c):
        return z * 8 + (x % 4) * 2 + c

    def unpack(p):
        return p // 8, (p // 2) % 4, p % 2

    def x_step(d):
        def f(p):
            z, x, c = unpack(p)
            return at(z, x + d, c)
        return f

    cross = moved(own, lambda p: p ^ 8)
    from_left = moved((own, cross), x_step(1))
    from_right = moved((own, cross), x_step(-1))
    far_own = moved(from_left[0], x_step(1))
    far_cross = moved(from_right[1], x_step(-1))
    mine = [
        (0, 0, own), (1, 0, cross),
        (0, -1, from_left[0]), (1, -1, from_left[1]),
        (0, 1, from_right[0]), (1, 1, from_right[1]),
        (0, 2, far_own), (1, 2, far_cross),
    ]
    other = moved(tuple(b for _, _, b in mine), lambda p: p ^ 1)
    width = own.shape[1]
    gathered = jnp.zeros((own.shape[0], 16 * width, own.shape[2]), own.dtype)
    for (dz, dx, block), far in zip(mine, other):
        for dc, piece in ((0, block), (1, far)):
            place = at((zh + dz) % 2, xx + dx + 4, (core + dc) % 2)
            gathered = lax.dynamic_update_slice(gathered, piece, (0, place * width, 0))
    return gathered


def shards(voltages, scales):
    inp_count = voltages.shape[0]
    shard_len = voltages.shape[1]
    spec_count = shard_len // NFFT
    history = TAPS - 1
    samples = voltages.reshape(inp_count, spec_count, NFFT).transpose(1, 0, 2).astype(jnp.bfloat16)
    earlier = []
    need = history
    distance = 1
    while need > 0:
        take = min(spec_count, need)
        earlier = [shifted(samples[spec_count - take :], TIME, distance)] + earlier
        need -= take
        distance += 1
    joined = jnp.concatenate(earlier + [samples], axis=0)
    gain = (scales.astype(jnp.float32) * (1.0 / 256.0)).reshape(inp_count, 1)
    filtered = polyphase(joined, window_table(), gain, spec_count).reshape(spec_count * inp_count, NFFT)
    spectra = jnp.dot(filtered, dft_table(), preferred_element_type=jnp.float32).astype(jnp.bfloat16)
    rows_y, rows_z = lax.axis_size("y"), lax.axis_size("zl")
    spectra = spectra.reshape(spec_count, inp_count, 2, rows_y, rows_z, CHANS // (rows_y * rows_z))
    step_z = lax.all_to_all(spectra, "zl", split_axis=4, concat_axis=0, tiled=True)
    step_y = lax.all_to_all(step_z, "y", split_axis=3, concat_axis=0, tiled=True)
    spec_total = step_y.shape[0]
    chan_count = step_y.shape[5]
    local_block = step_y.reshape(spec_total, inp_count, 2, chan_count)
    own_rows = local_block.transpose(3, 1, 2, 0).reshape(chan_count, inp_count, 2 * spec_total)
    swapped = jnp.concatenate([own_rows[..., spec_total:], -own_rows[..., :spec_total]], axis=-1)
    piece = gather_inputs(own_rows)
    real_part = jnp.einsum("cik,cjk->cij", own_rows, piece, preferred_element_type=jnp.float32)
    imag_part = jnp.einsum("cik,cjk->cij", swapped, piece, preferred_element_type=jnp.float32)
    result = jnp.stack([real_part, imag_part]) * (1.0 / spec_total)
    return result.astype(jnp.bfloat16)


def solution(mesh):
    fine = Mesh(mesh.devices.reshape(4, 8, 2, 4, 2), TIME + INPUT)
    placed = (P(INPUT, TIME), P(INPUT))
    inner = jax.shard_map(
        shards, mesh=fine, in_specs=placed, out_specs=P(None, TIME, INPUT, None), check_vma=False
    )
    target = NamedSharding(mesh, P(None, "chan", "inp", None))

    def run(voltages, scales):
        return jax.lax.with_sharding_constraint(inner(voltages, scales), target)

    return run
```

```python
import functools
import math

import jax
import jax.numpy as jnp
from jax import lax
from jax.experimental import pallas as pl
from jax.sharding import PartitionSpec as P

NFFT = 4096
CHANS = 1024
TAPS = 8
ROOT = 64


def shifted(block, axis, distance):
    devices = range(lax.axis_size(axis))
    route = [(i - distance, i) for i in devices if i - distance in devices]
    return lax.ppermute(block, axis, route)


def moved(block, mapping):
    return lax.ppermute(block, "inp", [(p, mapping(p)) for p in range(lax.axis_size("inp"))])


def window_table():
    count = TAPS * NFFT
    places = jnp.arange(count).astype(jnp.float32)
    shaping = jnp.sinc((places - count / 2.0) / NFFT)
    taper = 0.5 - 0.5 * jnp.cos(2.0 * math.pi * places / count)
    return (shaping * taper).reshape(TAPS, NFFT)


def dft_table():
    columns = jnp.arange(CHANS, dtype=jnp.int32)
    rows = jnp.arange(ROOT, dtype=jnp.int32)
    step = 2.0 * math.pi / NFFT

    def factor(scale):
        angle = ((scale * rows[:, None] * columns[None, :]) % NFFT).astype(jnp.float32) * step
        return jnp.cos(angle), -jnp.sin(angle)

    def spread(part, axis):
        grown = jnp.broadcast_to(jnp.expand_dims(part, axis), (ROOT, ROOT, CHANS))
        return grown.reshape(NFFT, CHANS)

    hr, hi = (spread(t, 1) for t in factor(ROOT))
    lr, li = (spread(t, 0) for t in factor(1))
    real = hr * lr - hi * li
    imag = hr * li + hi * lr
    both = jnp.concatenate([real, imag], axis=1) * (1.0 / math.sqrt(NFFT))
    return lax.optimization_barrier(both.astype(jnp.bfloat16))


def polyphase_kernel(spec_count, x_ref, w_ref, g_ref, o_ref):
    gain = g_ref[...]
    for s in range(spec_count):
        total = jnp.zeros(o_ref.shape[1:], jnp.float32)
        for tap in range(TAPS):
            total = total + w_ref[tap : tap + 1, :] * (x_ref[s + tap].astype(jnp.float32) * gain)
        o_ref[s] = total.astype(o_ref.dtype)


def polyphase(joined, window, gain, spec_count):
    rows, inputs, length = joined.shape
    lanes = 512
    return pl.pallas_call(
        functools.partial(polyphase_kernel, spec_count),
        out_shape=jax.ShapeDtypeStruct((spec_count, inputs, length), jnp.bfloat16),
        grid=(length // lanes,),
        in_specs=[
            pl.BlockSpec((rows, inputs, lanes), lambda k: (0, 0, k)),
            pl.BlockSpec((TAPS, lanes), lambda k: (0, k)),
            pl.BlockSpec((inputs, 1), lambda k: (0, 0)),
        ],
        out_specs=pl.BlockSpec((spec_count, inputs, lanes), lambda k: (0, 0, k)),
    )(joined, window, gain)


def gather_inputs(own):
    assert lax.axis_size("inp") == 16
    me = lax.axis_index("inp")
    zh, xx, core = me // 8, (me // 2) % 4, me % 2

    def at(z, x, c):
        return z * 8 + (x % 4) * 2 + c

    def x_step(d):
        return lambda p: at(p // 8, (p // 2) % 4 + d, p % 2)

    cross = moved(own, lambda p: p ^ 8)
    left_own = moved(own, x_step(1))
    right_own = moved(own, x_step(-1))
    far_own = moved(left_own, x_step(1))
    near = jnp.stack([own, left_own, right_own, far_own])
    near_other = moved(near, lambda p: p ^ 1)
    left_cross = moved(cross, x_step(1))
    right_cross = moved(cross, x_step(-1))
    far_cross = moved(right_cross, x_step(-1))
    far = jnp.stack([cross, left_cross, right_cross, far_cross])
    far_other = moved(far, lambda p: p ^ 1)
    width = own.shape[1]
    gathered = jnp.zeros((own.shape[0], 16 * width, own.shape[2]), own.dtype)
    sets = ((0, 0, near), (0, 1, near_other), (1, 0, far), (1, 1, far_other))
    for dz, dc, blocks in sets:
        for slot, dx in enumerate((0, -1, 1, 2)):
            place = at((zh + dz) % 2, xx + dx + 4, (core + dc) % 2)
            gathered = lax.dynamic_update_slice(gathered, blocks[slot], (0, place * width, 0))
    return gathered


def shards(voltages, scales):
    inp_count = voltages.shape[0]
    shard_len = voltages.shape[1]
    spec_count = shard_len // NFFT
    history = TAPS - 1
    samples = voltages.reshape(inp_count, spec_count, NFFT).transpose(1, 0, 2).astype(jnp.bfloat16)
    assert history <= 2 * spec_count
    recent = shifted(samples, "chan", 1)
    older = shifted(recent[2 * spec_count - history :], "chan", 1)
    earlier = [older, recent]
    joined = jnp.concatenate(earlier + [samples], axis=0)
    gain = (scales.astype(jnp.float32) * (1.0 / 256.0)).reshape(inp_count, 1)
    filtered = polyphase(joined, window_table(), gain, spec_count).reshape(spec_count * inp_count, NFFT)
    spectra = jnp.dot(filtered, dft_table(), preferred_element_type=jnp.float32).astype(jnp.bfloat16)
    spectra = spectra.reshape(spec_count, inp_count, 2, CHANS)
    local_block = lax.all_to_all(spectra, "chan", split_axis=3, concat_axis=0, tiled=True)
    spec_total = local_block.shape[0]
    chan_count = local_block.shape[3]
    own_rows = local_block.transpose(3, 1, 2, 0).reshape(chan_count, inp_count, 2 * spec_total)
    swapped = jnp.concatenate([own_rows[..., spec_total:], -own_rows[..., :spec_total]], axis=-1)
    piece = gather_inputs(own_rows)
    real_part = jnp.einsum("cik,cjk->cij", own_rows, piece, preferred_element_type=jnp.float32)
    imag_part = jnp.einsum("cik,cjk->cij", swapped, piece, preferred_element_type=jnp.float32)
    result = jnp.stack([real_part, imag_part]) * (1.0 / spec_total)
    return result.astype(jnp.bfloat16)


def solution(mesh):
    placed = (P("inp", "chan"), P("inp"))
    return jax.shard_map(
        shards, mesh=mesh, in_specs=placed, out_specs=P(None, "chan", "inp", None), check_vma=False
    )
```

```python
import functools
import math

import jax
import jax.numpy as jnp
from jax import lax
from jax.experimental import pallas as pl
from jax.sharding import Mesh, NamedSharding, PartitionSpec as P

NFFT = 4096
CHANS = 1024
TAPS = 8
ROOT = 64


TIME = ("y", "zl")
INPUT = ("zh", "x", "core")


def shifted(block, axis, distance):
    devices = range(lax.axis_size(axis))
    route = [(i - distance, i) for i in devices if i - distance in devices]
    return lax.ppermute(block, axis, route)


def moved(block, mapping):
    return lax.ppermute(block, INPUT, [(p, mapping(p)) for p in range(lax.axis_size(INPUT))])


def window_table():
    count = TAPS * NFFT
    places = jnp.arange(count).astype(jnp.float32)
    shaping = jnp.sinc((places - count / 2.0) / NFFT)
    taper = 0.5 - 0.5 * jnp.cos(2.0 * math.pi * places / count)
    return (shaping * taper).reshape(TAPS, NFFT)


def dft_table():
    columns = jnp.arange(CHANS, dtype=jnp.int32)
    rows = jnp.arange(ROOT, dtype=jnp.int32)
    step = 2.0 * math.pi / NFFT

    def factor(scale):
        angle = ((scale * rows[:, None] * columns[None, :]) % NFFT).astype(jnp.float32) * step
        return jnp.cos(angle), -jnp.sin(angle)

    def spread(part, axis):
        grown = jnp.broadcast_to(jnp.expand_dims(part, axis), (ROOT, ROOT, CHANS))
        return grown.reshape(NFFT, CHANS)

    hr, hi = (spread(t, 1) for t in factor(ROOT))
    lr, li = (spread(t, 0) for t in factor(1))
    real = hr * lr - hi * li
    imag = hr * li + hi * lr
    both = jnp.concatenate([real, imag], axis=1) * (1.0 / math.sqrt(NFFT))
    return lax.optimization_barrier(both.astype(jnp.bfloat16))


def polyphase_kernel(spec_count, x_ref, w_ref, g_ref, o_ref):
    gain = g_ref[...]
    for s in range(spec_count):
        total = jnp.zeros(o_ref.shape[1:], jnp.float32)
        for tap in range(TAPS):
            total = total + w_ref[tap : tap + 1, :] * (x_ref[s + tap].astype(jnp.float32) * gain)
        o_ref[s] = total.astype(o_ref.dtype)


def polyphase(joined, window, gain, spec_count):
    rows, inputs, length = joined.shape
    lanes = 512
    return pl.pallas_call(
        functools.partial(polyphase_kernel, spec_count),
        out_shape=jax.ShapeDtypeStruct((spec_count, inputs, length), jnp.bfloat16),
        grid=(length // lanes,),
        in_specs=[
            pl.BlockSpec((rows, inputs, lanes), lambda k: (0, 0, k)),
            pl.BlockSpec((TAPS, lanes), lambda k: (0, k)),
            pl.BlockSpec((inputs, 1), lambda k: (0, 0)),
        ],
        out_specs=pl.BlockSpec((spec_count, inputs, lanes), lambda k: (0, 0, k)),
    )(joined, window, gain)


def gather_inputs(own):
    zh = lax.axis_index("zh")
    cross = lax.ppermute(own, "zh", [(0, 1), (1, 0)])
    low_first = zh == 0
    pair = jnp.concatenate([jnp.where(low_first, own, cross), jnp.where(low_first, cross, own)], axis=1)
    everyone = lax.all_gather(pair, ("x", "core"), axis=1, tiled=True)
    chans, depth = own.shape[0], own.shape[2]
    groups = lax.axis_size(("x", "core"))
    ordered = everyone.reshape(chans, groups, 2, own.shape[1], depth).transpose(0, 2, 1, 3, 4)
    return ordered.reshape(chans, 2 * groups * own.shape[1], depth)


def shards(voltages, scales):
    inp_count = voltages.shape[0]
    shard_len = voltages.shape[1]
    spec_count = shard_len // NFFT
    history = TAPS - 1
    samples = voltages.reshape(inp_count, spec_count, NFFT).transpose(1, 0, 2).astype(jnp.bfloat16)
    earlier = []
    need = history
    distance = 1
    while need > 0:
        take = min(spec_count, need)
        earlier = [shifted(samples[spec_count - take :], TIME, distance)] + earlier
        need -= take
        distance += 1
    joined = jnp.concatenate(earlier + [samples], axis=0)
    gain = (scales.astype(jnp.float32) * (1.0 / 256.0)).reshape(inp_count, 1)
    filtered = polyphase(joined, window_table(), gain, spec_count).reshape(spec_count * inp_count, NFFT)
    spectra = jnp.dot(filtered, dft_table(), preferred_element_type=jnp.float32).astype(jnp.bfloat16)
    spectra = spectra.reshape(spec_count, inp_count, 2, CHANS)
    local_block = lax.all_to_all(spectra, TIME, split_axis=3, concat_axis=0, tiled=True)
    spec_total = local_block.shape[0]
    chan_count = local_block.shape[3]
    own_rows = local_block.transpose(3, 1, 2, 0).reshape(chan_count, inp_count, 2 * spec_total)
    swapped = jnp.concatenate([own_rows[..., spec_total:], -own_rows[..., :spec_total]], axis=-1)
    piece = gather_inputs(own_rows)
    real_part = jnp.einsum("cik,cjk->cij", own_rows, piece, preferred_element_type=jnp.float32)
    imag_part = jnp.einsum("cik,cjk->cij", swapped, piece, preferred_element_type=jnp.float32)
    result = jnp.stack([real_part, imag_part]) * (1.0 / spec_total)
    return result.astype(jnp.bfloat16)


def solution(mesh):
    fine = Mesh(mesh.devices.reshape(4, 8, 2, 4, 2), TIME + INPUT)
    placed = (P(INPUT, TIME), P(INPUT))
    inner = jax.shard_map(
        shards, mesh=fine, in_specs=placed, out_specs=P(None, TIME, INPUT, None), check_vma=False
    )
    target = NamedSharding(mesh, P(None, "chan", "inp", None))

    def run(voltages, scales):
        return jax.lax.with_sharding_constraint(inner(voltages, scales), target)

    return run
```

```python
import functools
import math

import jax
import jax.numpy as jnp
from jax import lax
from jax.experimental import pallas as pl
from jax.sharding import PartitionSpec as P

NFFT = 4096
CHANS = 1024
TAPS = 8
ROOT = 64


def shifted(block, axis, distance):
    devices = range(lax.axis_size(axis))
    route = [(i - distance, i) for i in devices if i - distance in devices]
    return lax.ppermute(block, axis, route)


def moved(block, mapping):
    return lax.ppermute(block, "inp", [(p, mapping(p)) for p in range(lax.axis_size("inp"))])


def window_table():
    count = TAPS * NFFT
    places = jnp.arange(count).astype(jnp.float32)
    shaping = jnp.sinc((places - count / 2.0) / NFFT)
    taper = 0.5 - 0.5 * jnp.cos(2.0 * math.pi * places / count)
    return (shaping * taper).reshape(TAPS, NFFT)


def dft_table():
    columns = jnp.arange(CHANS, dtype=jnp.int32)
    rows = jnp.arange(ROOT, dtype=jnp.int32)
    step = 2.0 * math.pi / NFFT

    def factor(scale):
        angle = ((scale * rows[:, None] * columns[None, :]) % NFFT).astype(jnp.float32) * step
        return jnp.cos(angle), -jnp.sin(angle)

    def spread(part, axis):
        grown = jnp.broadcast_to(jnp.expand_dims(part, axis), (ROOT, ROOT, CHANS))
        return grown.reshape(NFFT, CHANS)

    hr, hi = (spread(t, 1) for t in factor(ROOT))
    lr, li = (spread(t, 0) for t in factor(1))
    real = hr * lr - hi * li
    imag = hr * li + hi * lr
    both = jnp.concatenate([real, imag], axis=1) * (1.0 / math.sqrt(NFFT))
    return lax.optimization_barrier(both.astype(jnp.bfloat16))


def polyphase_kernel(spec_count, *refs):
    pieces, (w_ref, g_ref, o_ref) = refs[:-3], refs[-3:]
    gain = g_ref[...]
    rows = [p[k].astype(jnp.float32) * gain for p in pieces for k in range(p.shape[0])]
    for s in range(spec_count):
        total = jnp.zeros(o_ref.shape[1:], jnp.float32)
        for tap in range(TAPS):
            total = total + w_ref[tap : tap + 1, :] * rows[s + tap]
        o_ref[s] = total.astype(o_ref.dtype)


def polyphase(pieces, window, gain, spec_count):
    inputs, length = pieces[0].shape[1:]
    lanes = 512
    return pl.pallas_call(
        functools.partial(polyphase_kernel, spec_count),
        out_shape=jax.ShapeDtypeStruct((spec_count, inputs, length), jnp.bfloat16),
        grid=(length // lanes,),
        in_specs=[pl.BlockSpec((p.shape[0], inputs, lanes), lambda k: (0, 0, k)) for p in pieces]
        + [
            pl.BlockSpec((TAPS, lanes), lambda k: (0, k)),
            pl.BlockSpec((inputs, 1), lambda k: (0, 0)),
        ],
        out_specs=pl.BlockSpec((spec_count, inputs, lanes), lambda k: (0, 0, k)),
    )(*pieces, window, gain)


def gather_inputs(own):
    assert lax.axis_size("inp") == 16
    me = lax.axis_index("inp")
    zh, xx, core = me // 8, (me // 2) % 4, me % 2

    def at(z, x, c):
        return z * 8 + (x % 4) * 2 + c

    def unpack(p):
        return p // 8, (p // 2) % 4, p % 2

    def x_step(d):
        def f(p):
            z, x, c = unpack(p)
            return at(z, x + d, c)
        return f

    cross = moved(own, lambda p: p ^ 8)
    from_left = moved((own, cross), x_step(1))
    from_right = moved((own, cross), x_step(-1))
    far_own = moved(from_left[0], x_step(1))
    far_cross = moved(from_right[1], x_step(-1))
    mine = [
        (0, 0, own), (1, 0, cross),
        (0, -1, from_left[0]), (1, -1, from_left[1]),
        (0, 1, from_right[0]), (1, 1, from_right[1]),
        (0, 2, far_own), (1, 2, far_cross),
    ]
    other = moved(tuple(b for _, _, b in mine), lambda p: p ^ 1)
    width = own.shape[1]
    gathered = jnp.zeros((own.shape[0], 16 * width, own.shape[2]), own.dtype)
    for (dz, dx, block), far in zip(mine, other):
        for dc, piece in ((0, block), (1, far)):
            place = at((zh + dz) % 2, xx + dx + 4, (core + dc) % 2)
            gathered = lax.dynamic_update_slice(gathered, piece, (0, place * width, 0))
    return gathered


def shards(voltages, scales):
    inp_count = voltages.shape[0]
    shard_len = voltages.shape[1]
    spec_count = shard_len // NFFT
    history = TAPS - 1
    samples = voltages.reshape(inp_count, spec_count, NFFT).transpose(1, 0, 2).astype(jnp.bfloat16)
    earlier = []
    need = history
    distance = 1
    while need > 0:
        take = min(spec_count, need)
        earlier = [shifted(samples[spec_count - take :], "chan", distance)] + earlier
        need -= take
        distance += 1
    gain = (scales.astype(jnp.float32) * (1.0 / 256.0)).reshape(inp_count, 1)
    filtered = polyphase(earlier + [samples], window_table(), gain, spec_count)
    filtered = filtered.reshape(spec_count * inp_count, NFFT)
    spectra = jnp.dot(filtered, dft_table(), preferred_element_type=jnp.float32).astype(jnp.bfloat16)
    spectra = spectra.reshape(spec_count, inp_count, 2, CHANS)
    local_block = lax.all_to_all(spectra, "chan", split_axis=3, concat_axis=0, tiled=True)
    spec_total = local_block.shape[0]
    chan_count = local_block.shape[3]
    own_rows = local_block.transpose(3, 1, 2, 0).reshape(chan_count, inp_count, 2 * spec_total)
    swapped = jnp.concatenate([own_rows[..., spec_total:], -own_rows[..., :spec_total]], axis=-1)
    piece = gather_inputs(own_rows)
    real_part = jnp.einsum("cik,cjk->cij", own_rows, piece, preferred_element_type=jnp.float32)
    imag_part = jnp.einsum("cik,cjk->cij", swapped, piece, preferred_element_type=jnp.float32)
    result = jnp.stack([real_part, imag_part]) * (1.0 / spec_total)
    return result.astype(jnp.bfloat16)


def solution(mesh):
    placed = (P("inp", "chan"), P("inp"))
    return jax.shard_map(
        shards, mesh=mesh, in_specs=placed, out_specs=P(None, "chan", "inp", None), check_vma=False
    )
```

```python
import functools
import math

import jax
import jax.numpy as jnp
from jax import lax
from jax.experimental import pallas as pl
from jax.sharding import PartitionSpec as P

NFFT = 4096
CHANS = 1024
TAPS = 8
ROOT = 64


def shifted(block, axis, distance):
    devices = range(lax.axis_size(axis))
    route = [(i - distance, i) for i in devices if i - distance in devices]
    return lax.ppermute(block, axis, route)


def moved(block, mapping):
    return lax.ppermute(block, "inp", [(p, mapping(p)) for p in range(lax.axis_size("inp"))])


def window_table():
    count = TAPS * NFFT
    places = jnp.arange(count).astype(jnp.float32)
    shaping = jnp.sinc((places - count / 2.0) / NFFT)
    taper = 0.5 - 0.5 * jnp.cos(2.0 * math.pi * places / count)
    return (shaping * taper).reshape(TAPS, NFFT)


def dft_table():
    columns = jnp.arange(CHANS, dtype=jnp.int32)
    rows = jnp.arange(ROOT, dtype=jnp.int32)
    step = 2.0 * math.pi / NFFT

    def factor(scale):
        angle = ((scale * rows[:, None] * columns[None, :]) % NFFT).astype(jnp.float32) * step
        return jnp.cos(angle), -jnp.sin(angle)

    def spread(part, axis):
        grown = jnp.broadcast_to(jnp.expand_dims(part, axis), (ROOT, ROOT, CHANS))
        return grown.reshape(NFFT, CHANS)

    hr, hi = (spread(t, 1) for t in factor(ROOT))
    lr, li = (spread(t, 0) for t in factor(1))
    real = hr * lr - hi * li
    imag = hr * li + hi * lr
    both = jnp.concatenate([real, imag], axis=1) * (1.0 / math.sqrt(NFFT))
    return lax.optimization_barrier(both.astype(jnp.bfloat16))


def polyphase_kernel(spec_count, *refs):
    pieces, (w_ref, g_ref, o_ref) = refs[:-3], refs[-3:]
    gain = g_ref[...]
    rows = [p[k].astype(jnp.float32) * gain for p in pieces for k in range(p.shape[0])]
    for s in range(spec_count):
        total = jnp.zeros(o_ref.shape[1:], jnp.float32)
        for tap in range(TAPS):
            total = total + w_ref[tap : tap + 1, :] * rows[s + tap]
        o_ref[s] = total.astype(o_ref.dtype)


def polyphase(pieces, window, gain, spec_count):
    inputs, length = pieces[0].shape[1:]
    lanes = 512
    return pl.pallas_call(
        functools.partial(polyphase_kernel, spec_count),
        out_shape=jax.ShapeDtypeStruct((spec_count, inputs, length), jnp.bfloat16),
        grid=(length // lanes,),
        in_specs=[pl.BlockSpec((p.shape[0], inputs, lanes), lambda k: (0, 0, k)) for p in pieces]
        + [
            pl.BlockSpec((TAPS, lanes), lambda k: (0, k)),
            pl.BlockSpec((inputs, 1), lambda k: (0, 0)),
        ],
        out_specs=pl.BlockSpec((spec_count, inputs, lanes), lambda k: (0, 0, k)),
    )(*pieces, window, gain)


def gather_inputs(own):
    assert lax.axis_size("inp") == 16
    me = lax.axis_index("inp")
    zh, xx, core = me // 8, (me // 2) % 4, me % 2

    def at(z, x, c):
        return z * 8 + (x % 4) * 2 + c

    def unpack(p):
        return p // 8, (p // 2) % 4, p % 2

    def x_step(d):
        def f(p):
            z, x, c = unpack(p)
            return at(z, x + d, c)
        return f

    cross = moved(own, lambda p: p ^ 8)
    from_left = moved((own, cross), x_step(1))
    from_right = moved((own, cross), x_step(-1))
    far_own = moved(from_left[0], x_step(1))
    far_cross = moved(from_right[1], x_step(-1))
    mine = [
        (0, 0, own), (1, 0, cross),
        (0, -1, from_left[0]), (1, -1, from_left[1]),
        (0, 1, from_right[0]), (1, 1, from_right[1]),
        (0, 2, far_own), (1, 2, far_cross),
    ]
    other = moved(tuple(b for _, _, b in mine), lambda p: p ^ 1)
    width = own.shape[1]
    gathered = jnp.zeros((own.shape[0], 16 * width, own.shape[2]), own.dtype)
    for (dz, dx, block), far in zip(mine, other):
        for dc, piece in ((0, block), (1, far)):
            place = at((zh + dz) % 2, xx + dx + 4, (core + dc) % 2)
            gathered = lax.dynamic_update_slice(gathered, piece, (0, place * width, 0))
    return gathered


def shards(voltages, scales):
    inp_count = voltages.shape[0]
    shard_len = voltages.shape[1]
    spec_count = shard_len // NFFT
    history = TAPS - 1
    samples = voltages.reshape(inp_count, spec_count, NFFT).transpose(1, 0, 2).astype(jnp.bfloat16)
    behind = history - spec_count
    assert 0 <= behind <= spec_count
    count = lax.axis_size("chan")
    last = lax.axis_index("chan") == count - 1
    from_prev = shifted(samples[spec_count - behind :], "chan", 1)
    from_next = lax.ppermute(samples, "chan", [(i, (i - 1) % count) for i in range(count)])
    earlier = [jnp.where(last, jnp.zeros_like(from_prev), from_prev), jnp.where(last, jnp.zeros_like(samples), samples)]
    samples = from_next
    gain = (scales.astype(jnp.float32) * (1.0 / 256.0)).reshape(inp_count, 1)
    filtered = polyphase(earlier + [samples], window_table(), gain, spec_count)
    filtered = filtered.reshape(spec_count * inp_count, NFFT)
    spectra = jnp.dot(filtered, dft_table(), preferred_element_type=jnp.float32).astype(jnp.bfloat16)
    spectra = spectra.reshape(spec_count, inp_count, 2, CHANS)
    local_block = lax.all_to_all(spectra, "chan", split_axis=3, concat_axis=0, tiled=True)
    spec_total = local_block.shape[0]
    chan_count = local_block.shape[3]
    own_rows = local_block.transpose(3, 1, 2, 0).reshape(chan_count, inp_count, 2 * spec_total)
    swapped = jnp.concatenate([own_rows[..., spec_total:], -own_rows[..., :spec_total]], axis=-1)
    piece = gather_inputs(own_rows)
    real_part = jnp.einsum("cik,cjk->cij", own_rows, piece, preferred_element_type=jnp.float32)
    imag_part = jnp.einsum("cik,cjk->cij", swapped, piece, preferred_element_type=jnp.float32)
    result = jnp.stack([real_part, imag_part]) * (1.0 / spec_total)
    return result.astype(jnp.bfloat16)


def solution(mesh):
    placed = (P("inp", "chan"), P("inp"))
    return jax.shard_map(
        shards, mesh=mesh, in_specs=placed, out_specs=P(None, "chan", "inp", None), check_vma=False
    )
```

```python
import functools
import math

import jax
import jax.numpy as jnp
from jax import lax
from jax.experimental import pallas as pl
from jax.sharding import PartitionSpec as P

NFFT = 4096
CHANS = 1024
TAPS = 8
ROOT = 64


def shifted(block, axis, distance):
    devices = range(lax.axis_size(axis))
    route = [(i - distance, i) for i in devices if i - distance in devices]
    return lax.ppermute(block, axis, route)


def moved(block, mapping):
    return lax.ppermute(block, "inp", [(p, mapping(p)) for p in range(lax.axis_size("inp"))])


def window_table():
    count = TAPS * NFFT
    places = jnp.arange(count).astype(jnp.float32)
    shaping = jnp.sinc((places - count / 2.0) / NFFT)
    taper = 0.5 - 0.5 * jnp.cos(2.0 * math.pi * places / count)
    return (shaping * taper).reshape(TAPS, NFFT)


def dft_table():
    columns = jnp.arange(CHANS, dtype=jnp.int32)
    rows = jnp.arange(ROOT, dtype=jnp.int32)
    step = 2.0 * math.pi / NFFT

    def factor(scale):
        angle = ((scale * rows[:, None] * columns[None, :]) % NFFT).astype(jnp.float32) * step
        return jnp.cos(angle), -jnp.sin(angle)

    def spread(part, axis):
        grown = jnp.broadcast_to(jnp.expand_dims(part, axis), (ROOT, ROOT, CHANS))
        return grown.reshape(NFFT, CHANS)

    hr, hi = (spread(t, 1) for t in factor(ROOT))
    lr, li = (spread(t, 0) for t in factor(1))
    real = hr * lr - hi * li
    imag = hr * li + hi * lr
    both = jnp.concatenate([real, imag], axis=1) * (1.0 / math.sqrt(NFFT))
    return lax.optimization_barrier(both.astype(jnp.bfloat16))


def polyphase_kernel(spec_count, *refs):
    pieces, (w_ref, g_ref, o_ref) = refs[:-3], refs[-3:]
    gain = g_ref[...]
    rows = [p[k].astype(jnp.float32) * gain for p in pieces for k in range(p.shape[0])]
    for s in range(spec_count):
        total = jnp.zeros(o_ref.shape[1:], jnp.float32)
        for tap in range(TAPS):
            total = total + w_ref[tap : tap + 1, :] * rows[s + tap]
        o_ref[s] = total.astype(o_ref.dtype)


def polyphase(pieces, window, gain, spec_count):
    inputs, length = pieces[0].shape[1:]
    lanes = 512
    return pl.pallas_call(
        functools.partial(polyphase_kernel, spec_count),
        out_shape=jax.ShapeDtypeStruct((spec_count, inputs, length), jnp.bfloat16),
        grid=(length // lanes,),
        in_specs=[pl.BlockSpec((p.shape[0], inputs, lanes), lambda k: (0, 0, k)) for p in pieces]
        + [
            pl.BlockSpec((TAPS, lanes), lambda k: (0, k)),
            pl.BlockSpec((inputs, 1), lambda k: (0, 0)),
        ],
        out_specs=pl.BlockSpec((spec_count, inputs, lanes), lambda k: (0, 0, k)),
    )(*pieces, window, gain)


def gather_inputs(own, cross):
    assert lax.axis_size("inp") == 16
    me = lax.axis_index("inp")
    zh, xx, core = me // 8, (me // 2) % 4, me % 2

    def at(z, x, c):
        return z * 8 + (x % 4) * 2 + c

    def x_step(d):
        return lambda p: at(p // 8, (p // 2) % 4 + d, p % 2)

    from_left = moved((own, cross), x_step(1))
    from_right = moved((own, cross), x_step(-1))
    far_own = moved(from_left[0], x_step(1))
    far_cross = moved(from_right[1], x_step(-1))
    mine = [
        (0, 0, own), (1, 0, cross),
        (0, -1, from_left[0]), (1, -1, from_left[1]),
        (0, 1, from_right[0]), (1, 1, from_right[1]),
        (0, 2, far_own), (1, 2, far_cross),
    ]
    other = moved(tuple(b for _, _, b in mine), lambda p: p ^ 1)
    width = own.shape[1]
    gathered = jnp.zeros((own.shape[0], 16 * width, own.shape[2]), own.dtype)
    for (dz, dx, block), far in zip(mine, other):
        for dc, piece in ((0, block), (1, far)):
            place = at((zh + dz) % 2, xx + dx + 4, (core + dc) % 2)
            gathered = lax.dynamic_update_slice(gathered, piece, (0, place * width, 0))
    return gathered


def shards(voltages, scales):
    inp_count = voltages.shape[0]
    shard_len = voltages.shape[1]
    spec_count = shard_len // NFFT
    history = TAPS - 1
    samples = voltages.reshape(inp_count, spec_count, NFFT).transpose(1, 0, 2).astype(jnp.bfloat16)
    behind = history - spec_count
    assert 0 <= behind <= spec_count
    count = lax.axis_size("chan")
    last = lax.axis_index("chan") == count - 1
    from_prev = shifted(samples[spec_count - behind :], "chan", 1)
    from_next = lax.ppermute(samples, "chan", [(i, (i - 1) % count) for i in range(count)])
    earlier = [jnp.where(last, jnp.zeros_like(from_prev), from_prev), jnp.where(last, jnp.zeros_like(samples), samples)]
    samples = from_next
    gain = (scales.astype(jnp.float32) * (1.0 / 256.0)).reshape(inp_count, 1)
    filtered = polyphase(earlier + [samples], window_table(), gain, spec_count)
    filtered = filtered.reshape(spec_count * inp_count, NFFT)
    spectra = jnp.dot(filtered, dft_table(), preferred_element_type=jnp.float32).astype(jnp.bfloat16)
    spectra = spectra.reshape(spec_count, inp_count, 2, CHANS)
    crossed = moved(spectra, lambda p: p ^ 8)

    def corner_turn(block):
        turned = lax.all_to_all(block, "chan", split_axis=3, concat_axis=0, tiled=True)
        return turned.transpose(3, 1, 2, 0).reshape(turned.shape[3], inp_count, 2 * turned.shape[0])

    own_rows = corner_turn(spectra)
    spec_total = own_rows.shape[2] // 2
    swapped = jnp.concatenate([own_rows[..., spec_total:], -own_rows[..., :spec_total]], axis=-1)
    piece = gather_inputs(own_rows, corner_turn(crossed))
    real_part = jnp.einsum("cik,cjk->cij", own_rows, piece, preferred_element_type=jnp.float32)
    imag_part = jnp.einsum("cik,cjk->cij", swapped, piece, preferred_element_type=jnp.float32)
    result = jnp.stack([real_part, imag_part]) * (1.0 / spec_total)
    return result.astype(jnp.bfloat16)


def solution(mesh):
    placed = (P("inp", "chan"), P("inp"))
    return jax.shard_map(
        shards, mesh=mesh, in_specs=placed, out_specs=P(None, "chan", "inp", None), check_vma=False
    )
```

```python
import functools
import math

import jax
import jax.numpy as jnp
from jax import lax
from jax.experimental import pallas as pl
from jax.sharding import PartitionSpec as P

NFFT = 4096
CHANS = 1024
TAPS = 8
ROOT = 64


def shifted(block, axis, distance):
    devices = range(lax.axis_size(axis))
    route = [(i - distance, i) for i in devices if i - distance in devices]
    return lax.ppermute(block, axis, route)


def moved(block, mapping):
    return lax.ppermute(block, "inp", [(p, mapping(p)) for p in range(lax.axis_size("inp"))])


def window_table():
    count = TAPS * NFFT
    places = jnp.arange(count).astype(jnp.float32)
    shaping = jnp.sinc((places - count / 2.0) / NFFT)
    taper = 0.5 - 0.5 * jnp.cos(2.0 * math.pi * places / count)
    return (shaping * taper).reshape(TAPS, NFFT)


def dft_table():
    columns = jnp.arange(CHANS, dtype=jnp.int32)
    rows = jnp.arange(ROOT, dtype=jnp.int32)
    step = 2.0 * math.pi / NFFT

    def factor(scale):
        angle = ((scale * rows[:, None] * columns[None, :]) % NFFT).astype(jnp.float32) * step
        return jnp.cos(angle), -jnp.sin(angle)

    def spread(part, axis):
        grown = jnp.broadcast_to(jnp.expand_dims(part, axis), (ROOT, ROOT, CHANS))
        return grown.reshape(NFFT, CHANS)

    hr, hi = (spread(t, 1) for t in factor(ROOT))
    lr, li = (spread(t, 0) for t in factor(1))
    real = hr * lr - hi * li
    imag = hr * li + hi * lr
    both = jnp.concatenate([real, imag], axis=1) * (1.0 / math.sqrt(NFFT))
    return lax.optimization_barrier(both.astype(jnp.bfloat16))


def polyphase_kernel(spec_count, *refs):
    pieces, (w_ref, g_ref, o_ref) = refs[:-3], refs[-3:]
    gain = g_ref[...]
    rows = [p[k].astype(jnp.float32) * gain for p in pieces for k in range(p.shape[0])]
    for s in range(spec_count):
        total = jnp.zeros(o_ref.shape[1:], jnp.float32)
        for tap in range(TAPS):
            total = total + w_ref[tap : tap + 1, :] * rows[s + tap]
        o_ref[s] = total.astype(o_ref.dtype)


def polyphase(pieces, window, gain, spec_count):
    inputs, length = pieces[0].shape[1:]
    lanes = 512
    return pl.pallas_call(
        functools.partial(polyphase_kernel, spec_count),
        out_shape=jax.ShapeDtypeStruct((spec_count, inputs, length), jnp.bfloat16),
        grid=(length // lanes,),
        in_specs=[pl.BlockSpec((p.shape[0], inputs, lanes), lambda k: (0, 0, k)) for p in pieces]
        + [
            pl.BlockSpec((TAPS, lanes), lambda k: (0, k)),
            pl.BlockSpec((inputs, 1), lambda k: (0, 0)),
        ],
        out_specs=pl.BlockSpec((spec_count, inputs, lanes), lambda k: (0, 0, k)),
    )(*pieces, window, gain)


def gather_inputs(own):
    assert lax.axis_size("inp") == 16
    me = lax.axis_index("inp")
    zh, xx, core = me // 8, (me // 2) % 4, me % 2

    def at(z, x, c):
        return z * 8 + (x % 4) * 2 + c

    def unpack(p):
        return p // 8, (p // 2) % 4, p % 2

    def x_step(d):
        def f(p):
            z, x, c = unpack(p)
            return at(z, x + d, c)
        return f

    width = own.shape[1]

    def place(gathered, blocks, dz, dc):
        for block, dx in zip(blocks, (0, -1, 1, 2)):
            slot = at((zh + dz) % 2, xx + dx + 4, (core + dc) % 2)
            gathered = lax.dynamic_update_slice(gathered, block, (0, slot * width, 0))
        return gathered

    cross = moved(own, lambda p: p ^ 8)
    left_own = moved(own, x_step(1))
    right_own = moved(own, x_step(-1))
    near = (own, left_own, right_own, moved(left_own, x_step(1)))
    gathered = jnp.zeros((own.shape[0], 16 * width, own.shape[2]), own.dtype)
    gathered = place(place(gathered, near, 0, 0), moved(near, lambda p: p ^ 1), 0, 1)
    gathered, cross = lax.optimization_barrier((gathered, cross))
    right_cross = moved(cross, x_step(-1))
    far = (cross, moved(cross, x_step(1)), right_cross, moved(right_cross, x_step(-1)))
    return place(place(gathered, far, 1, 0), moved(far, lambda p: p ^ 1), 1, 1)


def shards(voltages, scales):
    inp_count = voltages.shape[0]
    shard_len = voltages.shape[1]
    spec_count = shard_len // NFFT
    history = TAPS - 1
    samples = voltages.reshape(inp_count, spec_count, NFFT).transpose(1, 0, 2).astype(jnp.bfloat16)
    behind = history - spec_count
    assert 0 <= behind <= spec_count
    count = lax.axis_size("chan")
    last = lax.axis_index("chan") == count - 1
    from_prev = shifted(samples[spec_count - behind :], "chan", 1)
    from_next = lax.ppermute(samples, "chan", [(i, (i - 1) % count) for i in range(count)])
    earlier = [jnp.where(last, jnp.zeros_like(from_prev), from_prev), jnp.where(last, jnp.zeros_like(samples), samples)]
    samples = from_next
    gain = (scales.astype(jnp.float32) * (1.0 / 256.0)).reshape(inp_count, 1)
    filtered = polyphase(earlier + [samples], window_table(), gain, spec_count)
    filtered = filtered.reshape(spec_count * inp_count, NFFT)
    spectra = jnp.dot(filtered, dft_table(), preferred_element_type=jnp.float32).astype(jnp.bfloat16)
    spectra = spectra.reshape(spec_count, inp_count, 2, CHANS)
    local_block = lax.all_to_all(spectra, "chan", split_axis=3, concat_axis=0, tiled=True)
    spec_total = local_block.shape[0]
    chan_count = local_block.shape[3]
    own_rows = local_block.transpose(3, 1, 2, 0).reshape(chan_count, inp_count, 2 * spec_total)
    swapped = jnp.concatenate([own_rows[..., spec_total:], -own_rows[..., :spec_total]], axis=-1)
    piece = gather_inputs(own_rows)
    real_part = jnp.einsum("cik,cjk->cij", own_rows, piece, preferred_element_type=jnp.float32)
    imag_part = jnp.einsum("cik,cjk->cij", swapped, piece, preferred_element_type=jnp.float32)
    result = jnp.stack([real_part, imag_part]) * (1.0 / spec_total)
    return result.astype(jnp.bfloat16)


def solution(mesh):
    placed = (P("inp", "chan"), P("inp"))
    return jax.shard_map(
        shards, mesh=mesh, in_specs=placed, out_specs=P(None, "chan", "inp", None), check_vma=False
    )
```

```python
import functools
import math

import jax
import jax.numpy as jnp
from jax import lax
from jax.experimental import pallas as pl
from jax.sharding import PartitionSpec as P

NFFT = 4096
CHANS = 1024
TAPS = 8
ROOT = 64


def shifted(block, axis, distance):
    devices = range(lax.axis_size(axis))
    route = [(i - distance, i) for i in devices if i - distance in devices]
    return lax.ppermute(block, axis, route)


def moved(block, mapping):
    return lax.ppermute(block, "inp", [(p, mapping(p)) for p in range(lax.axis_size("inp"))])


def window_table():
    count = TAPS * NFFT
    places = jnp.arange(count).astype(jnp.float32)
    shaping = jnp.sinc((places - count / 2.0) / NFFT)
    taper = 0.5 - 0.5 * jnp.cos(2.0 * math.pi * places / count)
    return (shaping * taper).reshape(TAPS, NFFT)


def dft_table():
    columns = jnp.arange(CHANS, dtype=jnp.int32)
    rows = jnp.arange(ROOT, dtype=jnp.int32)
    step = 2.0 * math.pi / NFFT

    def factor(scale):
        angle = ((scale * rows[:, None] * columns[None, :]) % NFFT).astype(jnp.float32) * step
        return jnp.cos(angle), -jnp.sin(angle)

    def spread(part, axis):
        grown = jnp.broadcast_to(jnp.expand_dims(part, axis), (ROOT, ROOT, CHANS))
        return grown.reshape(NFFT, CHANS)

    hr, hi = (spread(t, 1) for t in factor(ROOT))
    lr, li = (spread(t, 0) for t in factor(1))
    real = hr * lr - hi * li
    imag = hr * li + hi * lr
    both = jnp.concatenate([real, imag], axis=1) * (1.0 / math.sqrt(NFFT))
    return lax.optimization_barrier(both.astype(jnp.bfloat16))


def polyphase_kernel(spec_count, *refs):
    pieces, (w_ref, g_ref, o_ref) = refs[:-3], refs[-3:]
    gain = g_ref[...]
    rows = [p[k].astype(jnp.float32) * gain for p in pieces for k in range(p.shape[0])]
    for s in range(spec_count):
        total = jnp.zeros(o_ref.shape[1:], jnp.float32)
        for tap in range(TAPS):
            total = total + w_ref[tap : tap + 1, :] * rows[s + tap]
        o_ref[s] = total.astype(o_ref.dtype)


def polyphase(pieces, window, gain, spec_count):
    inputs, length = pieces[0].shape[1:]
    lanes = 512
    return pl.pallas_call(
        functools.partial(polyphase_kernel, spec_count),
        out_shape=jax.ShapeDtypeStruct((spec_count, inputs, length), jnp.bfloat16),
        grid=(length // lanes,),
        in_specs=[pl.BlockSpec((p.shape[0], inputs, lanes), lambda k: (0, 0, k)) for p in pieces]
        + [
            pl.BlockSpec((TAPS, lanes), lambda k: (0, k)),
            pl.BlockSpec((inputs, 1), lambda k: (0, 0)),
        ],
        out_specs=pl.BlockSpec((spec_count, inputs, lanes), lambda k: (0, 0, k)),
    )(*pieces, window, gain)


def gather_inputs(own):
    assert lax.axis_size("inp") == 16
    me = lax.axis_index("inp")
    zh, xx, core = me // 8, (me // 2) % 4, me % 2

    def at(z, x, c):
        return z * 8 + (x % 4) * 2 + c

    def unpack(p):
        return p // 8, (p // 2) % 4, p % 2

    def x_step(d):
        def f(p):
            z, x, c = unpack(p)
            return at(z, x + d, c)
        return f

    cross = moved(own, lambda p: p ^ 8)
    from_left = moved((own, cross), x_step(1))
    from_right = moved((own, cross), x_step(-1))
    far_own = moved(from_left[0], x_step(1))
    far_cross = moved(from_right[1], x_step(-1))
    mine = [
        (0, 0, own), (1, 0, cross),
        (0, -1, from_left[0]), (1, -1, from_left[1]),
        (0, 1, from_right[0]), (1, 1, from_right[1]),
        (0, 2, far_own), (1, 2, far_cross),
    ]
    other = moved(tuple(b for _, _, b in mine), lambda p: p ^ 1)
    width = own.shape[1]
    gathered = jnp.zeros((own.shape[0], 16 * width, own.shape[2]), own.dtype)
    for (dz, dx, block), far in zip(mine, other):
        for dc, piece in ((0, block), (1, far)):
            place = at((zh + dz) % 2, xx + dx + 4, (core + dc) % 2)
            gathered = lax.dynamic_update_slice(gathered, piece, (0, place * width, 0))
    return gathered


def shards(voltages, scales):
    inp_count = voltages.shape[0]
    shard_len = voltages.shape[1]
    spec_count = shard_len // NFFT
    history = TAPS - 1
    samples = voltages.reshape(inp_count, spec_count, NFFT).transpose(1, 0, 2).astype(jnp.bfloat16)
    behind = history - spec_count
    assert 0 <= behind <= spec_count
    count = lax.axis_size("chan")
    last = lax.axis_index("chan") == count - 1
    from_prev = shifted(samples[spec_count - behind :], "chan", 1)
    from_next = lax.ppermute(samples, "chan", [(i, (i - 1) % count) for i in range(count)])
    earlier = [jnp.where(last, jnp.zeros_like(from_prev), from_prev), jnp.where(last, jnp.zeros_like(samples), samples)]
    samples = from_next
    gain = (scales.astype(jnp.float32) * (1.0 / 256.0)).reshape(inp_count, 1)
    filtered = polyphase(earlier + [samples], window_table(), gain, spec_count)
    filtered = filtered.reshape(spec_count * inp_count, NFFT)
    spectra = jnp.dot(filtered, dft_table(), preferred_element_type=jnp.float32).astype(jnp.bfloat16)
    spectra = spectra.reshape(spec_count, inp_count, 2, CHANS)
    local_block = lax.all_to_all(spectra, "chan", split_axis=3, concat_axis=0, tiled=True)
    spec_total = local_block.shape[0]
    chan_count = local_block.shape[3]
    own_rows = local_block.transpose(3, 1, 2, 0).reshape(chan_count, inp_count, 2 * spec_total)
    swapped = jnp.concatenate([own_rows[..., spec_total:], -own_rows[..., :spec_total]], axis=-1)
    piece = gather_inputs(own_rows)
    lhs = jnp.concatenate([own_rows, swapped], axis=1)
    both = jnp.einsum("cik,cjk->cij", lhs, piece, preferred_element_type=jnp.float32)
    result = both.reshape(chan_count, 2, inp_count, -1).transpose(1, 0, 2, 3) * (1.0 / spec_total)
    return result.astype(jnp.bfloat16)


def solution(mesh):
    placed = (P("inp", "chan"), P("inp"))
    return jax.shard_map(
        shards, mesh=mesh, in_specs=placed, out_specs=P(None, "chan", "inp", None), check_vma=False
    )
```

```python
import functools
import math

import jax
import jax.numpy as jnp
from jax import lax
from jax.experimental import pallas as pl
from jax.sharding import PartitionSpec as P

NFFT = 4096
CHANS = 1024
TAPS = 8
ROOT = 64


def shifted(block, axis, distance):
    devices = range(lax.axis_size(axis))
    route = [(i - distance, i) for i in devices if i - distance in devices]
    return lax.ppermute(block, axis, route)


def moved(block, mapping):
    return lax.ppermute(block, "inp", [(p, mapping(p)) for p in range(lax.axis_size("inp"))])


def window_table():
    count = TAPS * NFFT
    places = jnp.arange(count).astype(jnp.float32)
    shaping = jnp.sinc((places - count / 2.0) / NFFT)
    taper = 0.5 - 0.5 * jnp.cos(2.0 * math.pi * places / count)
    return (shaping * taper).reshape(TAPS, NFFT)


def dft_table():
    columns = jnp.arange(CHANS, dtype=jnp.int32)
    rows = jnp.arange(ROOT, dtype=jnp.int32)
    step = 2.0 * math.pi / NFFT

    def factor(scale):
        angle = ((scale * rows[:, None] * columns[None, :]) % NFFT).astype(jnp.float32) * step
        return jnp.cos(angle), -jnp.sin(angle)

    def spread(part, axis):
        grown = jnp.broadcast_to(jnp.expand_dims(part, axis), (ROOT, ROOT, CHANS))
        return grown.reshape(NFFT, CHANS)

    hr, hi = (spread(t, 1) for t in factor(ROOT))
    lr, li = (spread(t, 0) for t in factor(1))
    real = hr * lr - hi * li
    imag = hr * li + hi * lr
    both = jnp.concatenate([real, imag], axis=1) * (1.0 / math.sqrt(NFFT))
    return lax.optimization_barrier(both.astype(jnp.bfloat16))


def polyphase_kernel(spec_count, *refs):
    pieces, (w_ref, g_ref, o_ref) = refs[:-3], refs[-3:]
    gain = g_ref[...]
    rows = [p[k].astype(jnp.float32) * gain for p in pieces for k in range(p.shape[0])]
    for s in range(spec_count):
        total = jnp.zeros(o_ref.shape[1:], jnp.float32)
        for tap in range(TAPS):
            total = total + w_ref[tap : tap + 1, :] * rows[s + tap]
        o_ref[s] = total.astype(o_ref.dtype)


def polyphase(pieces, window, gain, spec_count):
    inputs, length = pieces[0].shape[1:]
    lanes = 2048
    return pl.pallas_call(
        functools.partial(polyphase_kernel, spec_count),
        out_shape=jax.ShapeDtypeStruct((spec_count, inputs, length), jnp.bfloat16),
        grid=(length // lanes,),
        in_specs=[pl.BlockSpec((p.shape[0], inputs, lanes), lambda k: (0, 0, k)) for p in pieces]
        + [
            pl.BlockSpec((TAPS, lanes), lambda k: (0, k)),
            pl.BlockSpec((inputs, 1), lambda k: (0, 0)),
        ],
        out_specs=pl.BlockSpec((spec_count, inputs, lanes), lambda k: (0, 0, k)),
    )(*pieces, window, gain)


def gather_inputs(own):
    assert lax.axis_size("inp") == 16
    me = lax.axis_index("inp")
    zh, xx, core = me // 8, (me // 2) % 4, me % 2

    def at(z, x, c):
        return z * 8 + (x % 4) * 2 + c

    def unpack(p):
        return p // 8, (p // 2) % 4, p % 2

    def x_step(d):
        def f(p):
            z, x, c = unpack(p)
            return at(z, x + d, c)
        return f

    cross = moved(own, lambda p: p ^ 8)
    from_left = moved((own, cross), x_step(1))
    from_right = moved((own, cross), x_step(-1))
    far_own = moved(from_left[0], x_step(1))
    far_cross = moved(from_right[1], x_step(-1))
    mine = [
        (0, 0, own), (1, 0, cross),
        (0, -1, from_left[0]), (1, -1, from_left[1]),
        (0, 1, from_right[0]), (1, 1, from_right[1]),
        (0, 2, far_own), (1, 2, far_cross),
    ]
    other = moved(tuple(b for _, _, b in mine), lambda p: p ^ 1)
    width = own.shape[1]
    gathered = jnp.zeros((own.shape[0], 16 * width, own.shape[2]), own.dtype)
    for (dz, dx, block), far in zip(mine, other):
        for dc, piece in ((0, block), (1, far)):
            place = at((zh + dz) % 2, xx + dx + 4, (core + dc) % 2)
            gathered = lax.dynamic_update_slice(gathered, piece, (0, place * width, 0))
    return gathered


def shards(voltages, scales):
    inp_count = voltages.shape[0]
    shard_len = voltages.shape[1]
    spec_count = shard_len // NFFT
    history = TAPS - 1
    samples = voltages.reshape(inp_count, spec_count, NFFT).transpose(1, 0, 2).astype(jnp.bfloat16)
    behind = history - spec_count
    assert 0 <= behind <= spec_count
    count = lax.axis_size("chan")
    last = lax.axis_index("chan") == count - 1
    from_prev = shifted(samples[spec_count - behind :], "chan", 1)
    from_next = lax.ppermute(samples, "chan", [(i, (i - 1) % count) for i in range(count)])
    earlier = [jnp.where(last, jnp.zeros_like(from_prev), from_prev), jnp.where(last, jnp.zeros_like(samples), samples)]
    samples = from_next
    gain = (scales.astype(jnp.float32) * (1.0 / 256.0)).reshape(inp_count, 1)
    filtered = polyphase(earlier + [samples], window_table(), gain, spec_count)
    filtered = filtered.reshape(spec_count * inp_count, NFFT)
    spectra = jnp.dot(filtered, dft_table(), preferred_element_type=jnp.float32).astype(jnp.bfloat16)
    spectra = spectra.reshape(spec_count, inp_count, 2, CHANS)
    local_block = lax.all_to_all(spectra, "chan", split_axis=3, concat_axis=0, tiled=True)
    spec_total = local_block.shape[0]
    chan_count = local_block.shape[3]
    own_rows = local_block.transpose(3, 1, 2, 0).reshape(chan_count, inp_count, 2 * spec_total)
    swapped = jnp.concatenate([own_rows[..., spec_total:], -own_rows[..., :spec_total]], axis=-1)
    piece = gather_inputs(own_rows)
    lhs = jnp.concatenate([own_rows, swapped], axis=1)
    both = jnp.einsum("cik,cjk->cij", lhs, piece, preferred_element_type=jnp.float32)
    result = both.reshape(chan_count, 2, inp_count, -1).transpose(1, 0, 2, 3) * (1.0 / spec_total)
    return result.astype(jnp.bfloat16)


def solution(mesh):
    placed = (P("inp", "chan"), P("inp"))
    return jax.shard_map(
        shards, mesh=mesh, in_specs=placed, out_specs=P(None, "chan", "inp", None), check_vma=False
    )
```

```python
import functools
import math

import jax
import jax.numpy as jnp
from jax import lax
from jax.experimental import pallas as pl
from jax.sharding import PartitionSpec as P

NFFT = 4096
CHANS = 1024
TAPS = 8
ROOT = 64


def shifted(block, axis, distance):
    devices = range(lax.axis_size(axis))
    route = [(i - distance, i) for i in devices if i - distance in devices]
    return lax.ppermute(block, axis, route)


def moved(block, mapping):
    return lax.ppermute(block, "inp", [(p, mapping(p)) for p in range(lax.axis_size("inp"))])


def window_table():
    count = TAPS * NFFT
    places = jnp.arange(count).astype(jnp.float32)
    shaping = jnp.sinc((places - count / 2.0) / NFFT)
    taper = 0.5 - 0.5 * jnp.cos(2.0 * math.pi * places / count)
    return (shaping * taper).reshape(TAPS, NFFT)


def dft_table():
    columns = jnp.arange(CHANS, dtype=jnp.int32)
    rows = jnp.arange(ROOT, dtype=jnp.int32)
    step = 2.0 * math.pi / NFFT

    def factor(scale):
        angle = ((scale * rows[:, None] * columns[None, :]) % NFFT).astype(jnp.float32) * step
        return jnp.cos(angle), -jnp.sin(angle)

    def spread(part, axis):
        grown = jnp.broadcast_to(jnp.expand_dims(part, axis), (ROOT, ROOT, CHANS))
        return grown.reshape(NFFT, CHANS)

    hr, hi = (spread(t, 1) for t in factor(ROOT))
    lr, li = (spread(t, 0) for t in factor(1))
    real = hr * lr - hi * li
    imag = hr * li + hi * lr
    both = jnp.concatenate([real, imag], axis=1) * (1.0 / math.sqrt(NFFT))
    return lax.optimization_barrier(both.astype(jnp.bfloat16))


def polyphase_kernel(spec_count, *refs):
    pieces, (w_ref, c_ref, g_ref, o_ref) = refs[:-4], refs[-4:]
    gains = [c_ref[...]] * (len(pieces) - 1) + [g_ref[...]]
    rows = [p[k].astype(jnp.float32) * g for p, g in zip(pieces, gains) for k in range(p.shape[0])]
    for s in range(spec_count):
        total = jnp.zeros(o_ref.shape[1:], jnp.float32)
        for tap in range(TAPS):
            total = total + w_ref[tap : tap + 1, :] * rows[s + tap]
        o_ref[s] = total.astype(o_ref.dtype)


def polyphase(pieces, window, context_gain, gain, spec_count):
    inputs, length = pieces[0].shape[1:]
    lanes = 2048
    return pl.pallas_call(
        functools.partial(polyphase_kernel, spec_count),
        out_shape=jax.ShapeDtypeStruct((spec_count, inputs, length), jnp.bfloat16),
        grid=(length // lanes,),
        in_specs=[pl.BlockSpec((p.shape[0], inputs, lanes), lambda k: (0, 0, k)) for p in pieces]
        + [
            pl.BlockSpec((TAPS, lanes), lambda k: (0, k)),
            pl.BlockSpec((inputs, 1), lambda k: (0, 0)),
            pl.BlockSpec((inputs, 1), lambda k: (0, 0)),
        ],
        out_specs=pl.BlockSpec((spec_count, inputs, lanes), lambda k: (0, 0, k)),
    )(*pieces, window, context_gain, gain)


def gather_inputs(own):
    assert lax.axis_size("inp") == 16
    me = lax.axis_index("inp")
    zh, xx, core = me // 8, (me // 2) % 4, me % 2

    def at(z, x, c):
        return z * 8 + (x % 4) * 2 + c

    def unpack(p):
        return p // 8, (p // 2) % 4, p % 2

    def x_step(d):
        def f(p):
            z, x, c = unpack(p)
            return at(z, x + d, c)
        return f

    cross = moved(own, lambda p: p ^ 8)
    from_left = moved((own, cross), x_step(1))
    from_right = moved((own, cross), x_step(-1))
    far_own = moved(from_left[0], x_step(1))
    far_cross = moved(from_right[1], x_step(-1))
    mine = [
        (0, 0, own), (1, 0, cross),
        (0, -1, from_left[0]), (1, -1, from_left[1]),
        (0, 1, from_right[0]), (1, 1, from_right[1]),
        (0, 2, far_own), (1, 2, far_cross),
    ]
    other = moved(tuple(b for _, _, b in mine), lambda p: p ^ 1)
    width = own.shape[1]
    gathered = jnp.zeros((own.shape[0], 16 * width, own.shape[2]), own.dtype)
    for (dz, dx, block), far in zip(mine, other):
        for dc, piece in ((0, block), (1, far)):
            place = at((zh + dz) % 2, xx + dx + 4, (core + dc) % 2)
            gathered = lax.dynamic_update_slice(gathered, piece, (0, place * width, 0))
    return gathered


def shards(voltages, scales):
    inp_count = voltages.shape[0]
    shard_len = voltages.shape[1]
    spec_count = shard_len // NFFT
    history = TAPS - 1
    samples = voltages.reshape(inp_count, spec_count, NFFT).transpose(1, 0, 2).astype(jnp.bfloat16)
    behind = history - spec_count
    assert 0 <= behind <= spec_count
    count = lax.axis_size("chan")
    last = lax.axis_index("chan") == count - 1
    from_prev = shifted(samples[spec_count - behind :], "chan", 1)
    from_next = lax.ppermute(samples, "chan", [(i, (i - 1) % count) for i in range(count)])
    gain = (scales.astype(jnp.float32) * (1.0 / 256.0)).reshape(inp_count, 1)
    context_gain = jnp.where(last, jnp.zeros_like(gain), gain)
    filtered = polyphase([from_prev, samples, from_next], window_table(), context_gain, gain, spec_count)
    filtered = filtered.reshape(spec_count * inp_count, NFFT)
    spectra = jnp.dot(filtered, dft_table(), preferred_element_type=jnp.float32).astype(jnp.bfloat16)
    spectra = spectra.reshape(spec_count, inp_count, 2, CHANS)
    local_block = lax.all_to_all(spectra, "chan", split_axis=3, concat_axis=0, tiled=True)
    spec_total = local_block.shape[0]
    chan_count = local_block.shape[3]
    own_rows = local_block.transpose(3, 1, 2, 0).reshape(chan_count, inp_count, 2 * spec_total)
    swapped = jnp.concatenate([own_rows[..., spec_total:], -own_rows[..., :spec_total]], axis=-1)
    piece = gather_inputs(own_rows)
    lhs = jnp.concatenate([own_rows, swapped], axis=1)
    both = jnp.einsum("cik,cjk->cij", lhs, piece, preferred_element_type=jnp.float32)
    result = both.reshape(chan_count, 2, inp_count, -1).transpose(1, 0, 2, 3) * (1.0 / spec_total)
    return result.astype(jnp.bfloat16)


def solution(mesh):
    placed = (P("inp", "chan"), P("inp"))
    return jax.shard_map(
        shards, mesh=mesh, in_specs=placed, out_specs=P(None, "chan", "inp", None), check_vma=False
    )
```

```python
import functools
import math

import jax
import jax.numpy as jnp
from jax import lax
from jax.experimental import pallas as pl
from jax.sharding import PartitionSpec as P

NFFT = 4096
CHANS = 1024
TAPS = 8
ROOT = 64


def shifted(block, axis, distance):
    devices = range(lax.axis_size(axis))
    route = [(i - distance, i) for i in devices if i - distance in devices]
    return lax.ppermute(block, axis, route)


def moved(block, mapping):
    return lax.ppermute(block, "inp", [(p, mapping(p)) for p in range(lax.axis_size("inp"))])


def window_table():
    count = TAPS * NFFT
    places = jnp.arange(count).astype(jnp.float32)
    shaping = jnp.sinc((places - count / 2.0) / NFFT)
    taper = 0.5 - 0.5 * jnp.cos(2.0 * math.pi * places / count)
    return (shaping * taper).reshape(TAPS, NFFT)


def dft_table():
    columns = jnp.arange(CHANS, dtype=jnp.int32)
    rows = jnp.arange(ROOT, dtype=jnp.int32)
    step = 2.0 * math.pi / NFFT

    def factor(scale):
        angle = ((scale * rows[:, None] * columns[None, :]) % NFFT).astype(jnp.float32) * step
        return jnp.cos(angle), -jnp.sin(angle)

    def spread(part, axis):
        grown = jnp.broadcast_to(jnp.expand_dims(part, axis), (ROOT, ROOT, CHANS))
        return grown.reshape(NFFT, CHANS)

    hr, hi = (spread(t, 1) for t in factor(ROOT))
    lr, li = (spread(t, 0) for t in factor(1))
    real = hr * lr - hi * li
    imag = hr * li + hi * lr
    both = jnp.concatenate([real, imag], axis=1) * (1.0 / math.sqrt(NFFT))
    return lax.optimization_barrier(both.astype(jnp.bfloat16))


def polyphase_kernel(spec_count, *refs):
    pieces, (w_ref, c_ref, g_ref, o_ref) = refs[:-4], refs[-4:]
    gains = [c_ref[...]] * (len(pieces) - 1) + [g_ref[...]]
    rows = [p[k].astype(jnp.float32) * g for p, g in zip(pieces, gains) for k in range(p.shape[0])]
    for s in range(spec_count):
        total = jnp.zeros(o_ref.shape[1:], jnp.float32)
        for tap in range(TAPS):
            total = total + w_ref[tap : tap + 1, :] * rows[s + tap]
        o_ref[s] = total.astype(o_ref.dtype)


def polyphase(pieces, window, context_gain, gain, spec_count):
    inputs, length = pieces[0].shape[1:]
    lanes = 1024
    return pl.pallas_call(
        functools.partial(polyphase_kernel, spec_count),
        out_shape=jax.ShapeDtypeStruct((spec_count, inputs, length), jnp.bfloat16),
        grid=(length // lanes,),
        in_specs=[pl.BlockSpec((p.shape[0], inputs, lanes), lambda k: (0, 0, k)) for p in pieces]
        + [
            pl.BlockSpec((TAPS, lanes), lambda k: (0, k)),
            pl.BlockSpec((inputs, 1), lambda k: (0, 0)),
            pl.BlockSpec((inputs, 1), lambda k: (0, 0)),
        ],
        out_specs=pl.BlockSpec((spec_count, inputs, lanes), lambda k: (0, 0, k)),
    )(*pieces, window, context_gain, gain)


def gather_inputs(own):
    assert lax.axis_size("inp") == 16
    me = lax.axis_index("inp")
    zh, xx, core = me // 8, (me // 2) % 4, me % 2

    def at(z, x, c):
        return z * 8 + (x % 4) * 2 + c

    def unpack(p):
        return p // 8, (p // 2) % 4, p % 2

    def x_step(d):
        def f(p):
            z, x, c = unpack(p)
            return at(z, x + d, c)
        return f

    cross = moved(own, lambda p: p ^ 8)
    from_left = moved((own, cross), x_step(1))
    from_right = moved((own, cross), x_step(-1))
    far_own = moved(from_left[0], x_step(1))
    far_cross = moved(from_right[1], x_step(-1))
    mine = [
        (0, 0, own), (1, 0, cross),
        (0, -1, from_left[0]), (1, -1, from_left[1]),
        (0, 1, from_right[0]), (1, 1, from_right[1]),
        (0, 2, far_own), (1, 2, far_cross),
    ]
    other = moved(tuple(b for _, _, b in mine), lambda p: p ^ 1)
    width = own.shape[1]
    gathered = jnp.zeros((own.shape[0], 16 * width, own.shape[2]), own.dtype)
    for (dz, dx, block), far in zip(mine, other):
        for dc, piece in ((0, block), (1, far)):
            place = at((zh + dz) % 2, xx + dx + 4, (core + dc) % 2)
            gathered = lax.dynamic_update_slice(gathered, piece, (0, place * width, 0))
    return gathered


def shards(voltages, scales):
    inp_count = voltages.shape[0]
    shard_len = voltages.shape[1]
    spec_count = shard_len // NFFT
    history = TAPS - 1
    samples = voltages.reshape(inp_count, spec_count, NFFT).transpose(1, 0, 2).astype(jnp.bfloat16)
    behind = history - spec_count
    assert 0 <= behind <= spec_count
    count = lax.axis_size("chan")
    last = lax.axis_index("chan") == count - 1
    from_prev = shifted(samples[spec_count - behind :], "chan", 1)
    from_next = lax.ppermute(samples, "chan", [(i, (i - 1) % count) for i in range(count)])
    gain = (scales.astype(jnp.float32) * (1.0 / 256.0)).reshape(inp_count, 1)
    context_gain = jnp.where(last, jnp.zeros_like(gain), gain)
    filtered = polyphase([from_prev, samples, from_next], window_table(), context_gain, gain, spec_count)
    filtered = filtered.reshape(spec_count * inp_count, NFFT)
    spectra = jnp.dot(filtered, dft_table(), preferred_element_type=jnp.float32).astype(jnp.bfloat16)
    spectra = spectra.reshape(spec_count, inp_count, 2, CHANS)
    local_block = lax.all_to_all(spectra, "chan", split_axis=3, concat_axis=0, tiled=True)
    spec_total = local_block.shape[0]
    chan_count = local_block.shape[3]
    own_rows = local_block.transpose(3, 1, 2, 0).reshape(chan_count, inp_count, 2 * spec_total)
    swapped = jnp.concatenate([own_rows[..., spec_total:], -own_rows[..., :spec_total]], axis=-1)
    piece = gather_inputs(own_rows)
    lhs = jnp.concatenate([own_rows, swapped], axis=1)
    both = jnp.einsum("cik,cjk->cij", lhs, piece, preferred_element_type=jnp.float32)
    result = both.reshape(chan_count, 2, inp_count, -1).transpose(1, 0, 2, 3) * (1.0 / spec_total)
    return result.astype(jnp.bfloat16)


def solution(mesh):
    placed = (P("inp", "chan"), P("inp"))
    return jax.shard_map(
        shards, mesh=mesh, in_specs=placed, out_specs=P(None, "chan", "inp", None), check_vma=False
    )
```

```python
import functools
import math

import jax
import jax.numpy as jnp
from jax import lax
from jax.experimental import pallas as pl
from jax.sharding import PartitionSpec as P

NFFT = 4096
CHANS = 1024
TAPS = 8
ROOT = 64


def shifted(block, axis, distance):
    devices = range(lax.axis_size(axis))
    route = [(i - distance, i) for i in devices if i - distance in devices]
    return lax.ppermute(block, axis, route)


def moved(block, mapping):
    return lax.ppermute(block, "inp", [(p, mapping(p)) for p in range(lax.axis_size("inp"))])


def window_table():
    count = TAPS * NFFT
    places = jnp.arange(count).astype(jnp.float32)
    shaping = jnp.sinc((places - count / 2.0) / NFFT)
    taper = 0.5 - 0.5 * jnp.cos(2.0 * math.pi * places / count)
    return (shaping * taper).reshape(TAPS, NFFT)


def dft_table():
    columns = jnp.arange(CHANS, dtype=jnp.int32)
    rows = jnp.arange(ROOT, dtype=jnp.int32)
    step = 2.0 * math.pi / NFFT

    def factor(scale):
        angle = ((scale * rows[:, None] * columns[None, :]) % NFFT).astype(jnp.float32) * step
        return jnp.cos(angle), -jnp.sin(angle)

    def spread(part, axis):
        grown = jnp.broadcast_to(jnp.expand_dims(part, axis), (ROOT, ROOT, CHANS))
        return grown.reshape(NFFT, CHANS)

    hr, hi = (spread(t, 1) for t in factor(ROOT))
    lr, li = (spread(t, 0) for t in factor(1))
    real = hr * lr - hi * li
    imag = hr * li + hi * lr
    both = jnp.concatenate([real, imag], axis=1) * (1.0 / math.sqrt(NFFT))
    return lax.optimization_barrier(both.astype(jnp.bfloat16))


def polyphase_kernel(spec_count, *refs):
    pieces, (w_ref, c_ref, g_ref, o_ref) = refs[:-4], refs[-4:]
    gains = [c_ref[...]] * (len(pieces) - 1) + [g_ref[...]]
    rows = [p[k].astype(jnp.float32) * g for p, g in zip(pieces, gains) for k in range(p.shape[0])]
    for s in range(spec_count):
        total = jnp.zeros(o_ref.shape[1:], jnp.float32)
        for tap in range(TAPS):
            total = total + w_ref[tap : tap + 1, :] * rows[s + tap]
        o_ref[s] = total.astype(o_ref.dtype)


def polyphase(pieces, window, context_gain, gain, spec_count):
    inputs, length = pieces[0].shape[1:]
    lanes = 4096
    return pl.pallas_call(
        functools.partial(polyphase_kernel, spec_count),
        out_shape=jax.ShapeDtypeStruct((spec_count, inputs, length), jnp.bfloat16),
        grid=(length // lanes,),
        in_specs=[pl.BlockSpec((p.shape[0], inputs, lanes), lambda k: (0, 0, k)) for p in pieces]
        + [
            pl.BlockSpec((TAPS, lanes), lambda k: (0, k)),
            pl.BlockSpec((inputs, 1), lambda k: (0, 0)),
            pl.BlockSpec((inputs, 1), lambda k: (0, 0)),
        ],
        out_specs=pl.BlockSpec((spec_count, inputs, lanes), lambda k: (0, 0, k)),
    )(*pieces, window, context_gain, gain)


def gather_inputs(own):
    assert lax.axis_size("inp") == 16
    me = lax.axis_index("inp")
    zh, xx, core = me // 8, (me // 2) % 4, me % 2

    def at(z, x, c):
        return z * 8 + (x % 4) * 2 + c

    def unpack(p):
        return p // 8, (p // 2) % 4, p % 2

    def x_step(d):
        def f(p):
            z, x, c = unpack(p)
            return at(z, x + d, c)
        return f

    cross = moved(own, lambda p: p ^ 8)
    from_left = moved((own, cross), x_step(1))
    from_right = moved((own, cross), x_step(-1))
    far_own = moved(from_left[0], x_step(1))
    far_cross = moved(from_right[1], x_step(-1))
    mine = [
        (0, 0, own), (1, 0, cross),
        (0, -1, from_left[0]), (1, -1, from_left[1]),
        (0, 1, from_right[0]), (1, 1, from_right[1]),
        (0, 2, far_own), (1, 2, far_cross),
    ]
    other = moved(tuple(b for _, _, b in mine), lambda p: p ^ 1)
    width = own.shape[1]
    gathered = jnp.zeros((own.shape[0], 16 * width, own.shape[2]), own.dtype)
    for (dz, dx, block), far in zip(mine, other):
        for dc, piece in ((0, block), (1, far)):
            place = at((zh + dz) % 2, xx + dx + 4, (core + dc) % 2)
            gathered = lax.dynamic_update_slice(gathered, piece, (0, place * width, 0))
    return gathered


def shards(voltages, scales):
    inp_count = voltages.shape[0]
    shard_len = voltages.shape[1]
    spec_count = shard_len // NFFT
    history = TAPS - 1
    samples = voltages.reshape(inp_count, spec_count, NFFT).transpose(1, 0, 2).astype(jnp.bfloat16)
    behind = history - spec_count
    assert 0 <= behind <= spec_count
    count = lax.axis_size("chan")
    last = lax.axis_index("chan") == count - 1
    from_prev = shifted(samples[spec_count - behind :], "chan", 1)
    from_next = lax.ppermute(samples, "chan", [(i, (i - 1) % count) for i in range(count)])
    gain = (scales.astype(jnp.float32) * (1.0 / 256.0)).reshape(inp_count, 1)
    context_gain = jnp.where(last, jnp.zeros_like(gain), gain)
    filtered = polyphase([from_prev, samples, from_next], window_table(), context_gain, gain, spec_count)
    filtered = filtered.reshape(spec_count * inp_count, NFFT)
    spectra = jnp.dot(filtered, dft_table(), preferred_element_type=jnp.float32).astype(jnp.bfloat16)
    spectra = spectra.reshape(spec_count, inp_count, 2, CHANS)
    local_block = lax.all_to_all(spectra, "chan", split_axis=3, concat_axis=0, tiled=True)
    spec_total = local_block.shape[0]
    chan_count = local_block.shape[3]
    own_rows = local_block.transpose(3, 1, 2, 0).reshape(chan_count, inp_count, 2 * spec_total)
    swapped = jnp.concatenate([own_rows[..., spec_total:], -own_rows[..., :spec_total]], axis=-1)
    piece = gather_inputs(own_rows)
    lhs = jnp.concatenate([own_rows, swapped], axis=1)
    both = jnp.einsum("cik,cjk->cij", lhs, piece, preferred_element_type=jnp.float32)
    result = both.reshape(chan_count, 2, inp_count, -1).transpose(1, 0, 2, 3) * (1.0 / spec_total)
    return result.astype(jnp.bfloat16)


def solution(mesh):
    placed = (P("inp", "chan"), P("inp"))
    return jax.shard_map(
        shards, mesh=mesh, in_specs=placed, out_specs=P(None, "chan", "inp", None), check_vma=False
    )
```
